128 devices in a mesh: req: 32 (over x, z, core), tensor: 4 (over y).
Axes of the slice: x: 4, y: 4, z: 4, core: 2. Of those that a mesh axis runs over, the one named last changes fastest.
Arguments:
- hidden_in: bfloat16 [32768, 2048], P('req', 'tensor'), may hold values from -6 to 6
- segment: int32 [32768], P('req'), may hold values from 0 to 15, never falling along the last dimension, each value on 1 to 4096 neighbouring positions
- w_query: bfloat16 [2048, 1024], P(None, 'tensor'), may hold values from -0.125 to 0.125
- w_key: bfloat16 [2048, 1024], P(None, 'tensor'), may hold values from -0.125 to 0.125
- w_value: bfloat16 [2048, 2048], P(None, 'tensor'), may hold values from -0.125 to 0.125
- w_outgate: bfloat16 [2048, 2048], P(None, 'tensor'), may hold values from -0.125 to 0.125
- w_gate_down: bfloat16 [2048, 16], replicated, may hold values from -0.125 to 0.125
- w_gate_up: bfloat16 [16, 1024], P(None, 'tensor'), may hold values from -1.5 to 1.5
- gate_bias: float32 [1024], P('tensor'), may hold values from -2 to 8
- norm_gain: float32 [512], replicated, may hold values from 0.5 to 1.5
- w_out: bfloat16 [2048, 2048], P('tensor'), may hold values from -0.125 to 0.125
Outputs:
- mixed: bfloat16 [32768, 2048], P('req', 'tensor')
The draws below stay inside these ranges and needn't reach their ends.
Inputs may be any that keep to these rules, and one draw needn't show every extreme that they name: segment never falls along the tokens; each prompt covers 1 to 4096 consecutive tokens and one covers exactly 4096.
All inputs are finite; a program needn't handle non-finite values.
Results may differ from the reference program's by a relative error of at most 0.014.
Values may be sent and summed in bfloat16 or wider, within the bound.
No kernel may reach another device: no remote copies, remote signals or barrier semaphores. Data moves between devices by JAX's collectives and lax.ppermute only.
A program may use at most 128 MiB of HBM per device.

```python
import math
import jax
import jax.numpy as jnp
import numpy as np
from jax import lax

D = 2048
HEADS = 4
DK = 256
DV = 512
RANK = 16
TOKENS = 32768
SEG_COUNT = 16
SEG_MOST = 4096


def steps_of(own_key, dims, pieces, low, high):
    gain = 1.0
    for axis_at, blocks in pieces:
        draws = jax.random.uniform(jax.random.fold_in(jax.random.fold_in(own_key, 6), axis_at), (blocks,), jnp.float32, low / len(pieces), high / len(pieces))
        gain = gain * jnp.repeat(jnp.exp(draws), dims[axis_at] // blocks).reshape((-1,) + (1,) * (len(dims) - 1 - axis_at))
    return gain


def profile(number_of, total, bound, slope):
    loads = [(1 << 20) // math.isqrt(rank ** slope) + 1 for rank in range(2, number_of + 1)]
    spare, counts = total - bound - (number_of - 1), [1] * (number_of - 1)
    while spare > 0:
        candidates = [i for i in range(number_of - 1) if counts[i] < bound]
        whole, budget = sum([loads[i] for i in candidates]), spare
        for i in candidates:
            more = min(bound - counts[i], max(1, budget * loads[i] // whole), spare)
            counts[i] = counts[i] + more
            spare = spare - more
    return np.array([bound] + counts)


def ragged(rng, number_of, total, limit, slope):
    if number_of == 2:
        one = jax.random.randint(rng, (), max(1, total - limit), min(limit, total - 1) + 1)
        return jnp.stack([one, total - one])
    lengths = jnp.asarray(profile(number_of, total, limit, slope), jnp.int32)
    pairs = (number_of - 1) // 2
    giver, taker = lengths[1:1 + 2 * pairs:2], lengths[2:2 + 2 * pairs:2]
    slack = jnp.minimum(giver - 1, limit - taker)
    passed = jax.random.randint(jax.random.fold_in(rng, 1), (pairs,), 0, 1 << 20) % (slack + 1)
    lengths = lengths.at[1:1 + 2 * pairs:2].set(giver - passed).at[2:2 + 2 * pairs:2].set(taker + passed)
    return lengths[jax.random.permutation(jax.random.fold_in(rng, 2), number_of)]


def centred(rng, shape, spread, bound, pieces=(), held_as=jnp.bfloat16):
    entries = jax.random.normal(rng, shape, jnp.float32) * spread
    if len(pieces) > 0:
        entries = steps_of(rng, shape, pieces, -0.22, 0.18) * entries
    return jnp.clip(entries, min=-bound, max=bound).astype(held_as)


def setup_inputs(seed: int = 0) -> dict:
    key_list = jax.random.split(jax.random.key(seed), 12)
    hidden_in = centred(key_list[0], (TOKENS, D), 1.0, 6.0, ((0, 32), (1, 4)))
    segment = jnp.searchsorted(jnp.cumsum(ragged(key_list[1], SEG_COUNT, TOKENS, SEG_MOST, 2)), jnp.arange(TOKENS), side="right").astype(jnp.int32)
    w_query = centred(key_list[2], (D, HEADS * DK), D ** -0.5, 0.125, ((1, 4),))
    w_key = centred(key_list[3], (D, HEADS * DK), D ** -0.5, 0.125, ((1, 4),))
    w_value = centred(key_list[4], (D, HEADS * DV), D ** -0.5, 0.125, ((1, 4),))
    w_outgate = centred(key_list[5], (D, HEADS * DV), D ** -0.5, 0.125, ((1, 4),))
    w_gate_down = centred(key_list[6], (D, RANK), D ** -0.5, 0.125)
    w_gate_up = centred(key_list[7], (RANK, HEADS * DK), RANK ** -0.5, 1.5, ((1, 4),))
    gate_bias = jnp.clip(-2.0 + 10.0 * jax.random.uniform(key_list[8], (HEADS * DK,), jnp.float32) ** steps_of(key_list[8], (HEADS * DK,), ((0, 4),), -0.2, 0.2), -2.0, 8.0)
    norm_gain = jnp.clip(1.0 + 0.1 * jax.random.normal(key_list[9], (DV,), jnp.float32), 0.5, 1.5)
    w_out = centred(key_list[10], (HEADS * DV, D), (HEADS * DV) ** -0.5, 0.125, ((0, 4),))
    return {"hidden_in": hidden_in, "segment": segment, "w_query": w_query, "w_key": w_key, "w_value": w_value, "w_outgate": w_outgate, "w_gate_down": w_gate_down, "w_gate_up": w_gate_up, "gate_bias": gate_bias, "norm_gain": norm_gain, "w_out": w_out}


def reference(hidden_in, segment, w_query, w_key, w_value, w_outgate, w_gate_down, w_gate_up, gate_bias, norm_gain, w_out):
    count_rows = hidden_in.shape[0]
    query = jnp.dot(hidden_in, w_query, preferred_element_type=jnp.float32).astype(jnp.bfloat16)
    key = jnp.dot(hidden_in, w_key, preferred_element_type=jnp.float32).astype(jnp.bfloat16)
    value = jnp.dot(hidden_in, w_value, preferred_element_type=jnp.float32).astype(jnp.bfloat16)
    outgate = jnp.dot(hidden_in, w_outgate, preferred_element_type=jnp.float32)
    low = jnp.dot(hidden_in, w_gate_down, preferred_element_type=jnp.float32)
    pre_gate = jnp.dot(low, w_gate_up.astype(jnp.float32), precision=lax.Precision.HIGHEST) + gate_bias
    logdecay = jax.nn.log_sigmoid(pre_gate) / 16.0
    same = jnp.concatenate([jnp.zeros((1,), jnp.float32), (segment[1:] == segment[:-1]).astype(jnp.float32)])
    query_heads = query.astype(jnp.float32).reshape(count_rows, HEADS, DK)
    key_heads = key.astype(jnp.float32).reshape(count_rows, HEADS, DK)
    value_heads = value.astype(jnp.float32).reshape(count_rows, HEADS, DV)
    decay_heads = jnp.exp(logdecay).reshape(count_rows, HEADS, DK)

    def advance(state, inputs):
        q_row, k_row, v_row, d_row, s_row = inputs
        state = state * (d_row * s_row)[:, :, None] + k_row[:, :, None] * v_row[:, None, :]
        result = jnp.einsum('hc,hcv->hv', q_row, state, precision=lax.Precision.HIGHEST)
        return (state, result)
    start_state = jnp.zeros((HEADS, DK, DV), jnp.float32)
    final_state, attn = lax.scan(advance, start_state, (query_heads, key_heads, value_heads, decay_heads, same))
    attn = attn * DK ** (-0.5)
    normed = attn * lax.rsqrt(lax.optimization_barrier(jnp.mean(attn * attn, axis=-1, keepdims=True)) + 1e-05) * norm_gain
    gated = (normed * jax.nn.silu(outgate.reshape(count_rows, HEADS, DV))).astype(jnp.bfloat16)
    total = jnp.zeros((count_rows, D), jnp.float32)
    for head in range(HEADS):
        term = jnp.dot(gated[:, head, :], w_out[head * DV:(head + 1) * DV], preferred_element_type=jnp.float32)
        total = total + term.astype(jnp.bfloat16).astype(jnp.float32)
    return total.astype(jnp.bfloat16)
```

```python
import jax
import jax.numpy as jnp
from jax import lax
from jax.sharding import PartitionSpec as P

GROUP = 64
SEG_MOST = 4096
HIGHEST = lax.Precision.HIGHEST


def shifted(x, axis, shift, devices):
    pairs = [(i, i + shift) for i in range(devices - shift)]
    return lax.ppermute(x, axis, pairs)


def body(
    hidden_in,
    segment,
    w_query,
    w_key,
    w_value,
    w_outgate,
    w_gate_down,
    w_gate_up,
    gate_bias,
    norm_gain,
    w_out,
):
    tok_rows = hidden_in.shape[0]
    key_width = w_query.shape[1]
    value_width = w_value.shape[1]
    weights = (w_query, w_key, w_value, w_outgate, w_gate_down)
    piece = lax.all_gather(hidden_in, "tensor", axis=1, tiled=True)
    query_sum, key_sum, value_sum, outgate, low = tuple(
        (jnp.dot(piece, weight, preferred_element_type=jnp.float32) for weight in weights)
    )
    query = query_sum.astype(jnp.bfloat16)
    key = key_sum.astype(jnp.bfloat16)
    value = value_sum.astype(jnp.bfloat16)
    pre_gate = jnp.dot(low, w_gate_up.astype(jnp.float32), precision=HIGHEST) + gate_bias
    logdecay = jax.nn.log_sigmoid(pre_gate) / 16.0

    blocks = tok_rows // GROUP
    starts = jnp.concatenate(
        [jnp.zeros((1,), jnp.int32), (segment[1:] != segment[:-1]).astype(jnp.int32)]
    )
    live_device = (jnp.cumsum(starts) == 0).astype(jnp.float32)
    seg_blocks = segment.reshape(blocks, GROUP)
    live_blocks = (jnp.cumsum(starts.reshape(blocks, GROUP), axis=1) == 0).astype(jnp.float32)
    cumul = jnp.cumsum(logdecay.reshape(blocks, GROUP, key_width), axis=1)
    block_totals = cumul[:, -1, :]
    before = jnp.cumsum(block_totals, axis=0) - block_totals
    device_cumul = (cumul + before[:, None, :]).reshape(tok_rows, key_width)

    q_float = query.astype(jnp.float32).reshape(blocks, GROUP, key_width)
    k_float = key.astype(jnp.float32).reshape(blocks, GROUP, key_width)
    v_float = value.astype(jnp.float32).reshape(blocks, GROUP, value_width)

    positions = jnp.arange(GROUP)
    causal = positions[None, :] <= positions[:, None]
    centre = cumul[:, GROUP // 2, :]
    q_scaled = q_float * jnp.exp(cumul - centre[:, None, :])
    k_scaled = k_float * jnp.exp(centre[:, None, :] - cumul)
    raw_scores = jnp.einsum("ncd,nsd->ncs", q_scaled, k_scaled, precision=HIGHEST)
    allowed = causal[None] & (seg_blocks[:, :, None] == seg_blocks[:, None, :])
    scores = jnp.where(allowed, raw_scores, 0.0)
    intra = jnp.einsum("ncs,nsv->ncv", scores, v_float, precision=HIGHEST)

    same_last = (seg_blocks == seg_blocks[:, -1:]).astype(jnp.float32)
    k_decayed = k_float * jnp.exp(block_totals[:, None, :] - cumul) * same_last[:, :, None]
    chunk_states = jnp.einsum("ncd,ncv->ndv", k_decayed, v_float, precision=HIGHEST)
    chunk_decay = jnp.exp(block_totals) * live_blocks[:, -1:]

    entering = [jnp.zeros((key_width, value_width), jnp.float32)]
    for n in range(blocks):
        entering.append(chunk_decay[n][:, None] * entering[-1] + chunk_states[n])
    final_state = entering[-1]
    entering = jnp.stack(entering[:-1])
    inter = (
        jnp.einsum("ncd,ndv->ncv", q_float * jnp.exp(cumul), entering, precision=HIGHEST)
        * live_blocks[:, :, None]
    )
    local_out = (intra + inter).reshape(tok_rows, value_width)

    devices = lax.axis_size("req")
    window = min(devices - 1, -(-SEG_MOST // tok_rows))
    first_id = (segment[0] + 1).astype(jnp.float32)
    last_id = (segment[-1] + 1).astype(jnp.float32)
    decay_device = jnp.exp(device_cumul[-1]) * live_device[-1]
    ids = jnp.stack([first_id, last_id])
    sent_state = final_state.astype(jnp.bfloat16)
    got = [
        (
            shifted(ids, "req", j, devices),
            shifted(decay_device, "req", j, devices),
            shifted(sent_state, "req", j, devices).astype(jnp.float32),
        )
        for j in range(1, window + 1)
    ]
    ids_far, _, state_in = got[-1]
    for j in range(window - 1, 0, -1):
        ids_j, decay_j, state_j = got[j - 1]
        link = (ids_j[0] == ids_far[1]).astype(jnp.float32)
        state_in = state_j + (link * decay_j)[:, None] * state_in
        ids_far = ids_j
    linked = (first_id == ids_far[1]).astype(jnp.float32)
    carried = jnp.dot(
        query.astype(jnp.float32) * jnp.exp(device_cumul), state_in, precision=HIGHEST
    )
    attn = (local_out + carried * (live_device * linked)[:, None]) * key_width ** (-0.5)
    normed = attn * lax.rsqrt(jnp.mean(attn * attn, axis=-1, keepdims=True) + 1e-05) * norm_gain
    gated = (normed * jax.nn.silu(outgate)).astype(jnp.bfloat16)
    head_term = jnp.dot(gated, w_out, preferred_element_type=jnp.float32)
    return lax.psum_scatter(
        head_term.astype(jnp.bfloat16), "tensor", scatter_dimension=1, tiled=True
    )


def solution(mesh):
    in_specs = (
        P("req", "tensor"),
        P("req"),
        P(None, "tensor"),
        P(None, "tensor"),
        P(None, "tensor"),
        P(None, "tensor"),
        P(),
        P(None, "tensor"),
        P("tensor"),
        P(),
        P("tensor", None),
    )
    out_specs = P("req", "tensor")
    return jax.shard_map(body, mesh=mesh, in_specs=in_specs, out_specs=out_specs, check_vma=False)
```

```python
import jax
import jax.numpy as jnp
from jax import lax
from jax.sharding import PartitionSpec as P

GROUP = 64
PIECES = 4
SEG_MOST = 4096
HIGHEST = lax.Precision.HIGHEST


def shifted(x, axis, shift, devices):
    pairs = [(i, i + shift) for i in range(devices - shift)]
    return lax.ppermute(x, axis, pairs)


def body(
    hidden_in,
    segment,
    w_query,
    w_key,
    w_value,
    w_outgate,
    w_gate_down,
    w_gate_up,
    gate_bias,
    norm_gain,
    w_out,
):
    tok_rows = hidden_in.shape[0]
    key_width = w_query.shape[1]
    value_width = w_value.shape[1]
    weights = (w_query, w_key, w_value, w_outgate, w_gate_down)
    piece_rows = tok_rows // PIECES
    piece_blocks = piece_rows // GROUP
    blocks = tok_rows // GROUP
    positions = jnp.arange(GROUP)
    causal = positions[None, :] <= positions[:, None]

    starts = jnp.concatenate(
        [jnp.zeros((1,), jnp.int32), (segment[1:] != segment[:-1]).astype(jnp.int32)]
    )
    live_device = (jnp.cumsum(starts) == 0).astype(jnp.float32)
    seg_all = segment.reshape(blocks, GROUP)
    live_all = (jnp.cumsum(starts.reshape(blocks, GROUP), axis=1) == 0).astype(jnp.float32)

    parts = []
    for p in range(PIECES):
        rows = slice(p * piece_rows, (p + 1) * piece_rows)
        piece = lax.all_gather(hidden_in[rows], "tensor", axis=1, tiled=True)
        query_sum, key_sum, value_sum, outgate, low = tuple(
            (jnp.dot(piece, weight, preferred_element_type=jnp.float32) for weight in weights)
        )
        query = query_sum.astype(jnp.bfloat16)
        key = key_sum.astype(jnp.bfloat16)
        value = value_sum.astype(jnp.bfloat16)
        pre_gate = jnp.dot(low, w_gate_up.astype(jnp.float32), precision=HIGHEST) + gate_bias
        logdecay = jax.nn.log_sigmoid(pre_gate) / 16.0

        chunks = slice(p * piece_blocks, (p + 1) * piece_blocks)
        seg_blocks = seg_all[chunks]
        live_blocks = live_all[chunks]
        cumul = jnp.cumsum(logdecay.reshape(piece_blocks, GROUP, key_width), axis=1)
        q_float = query.astype(jnp.float32).reshape(piece_blocks, GROUP, key_width)
        k_float = key.astype(jnp.float32).reshape(piece_blocks, GROUP, key_width)
        v_float = value.astype(jnp.float32).reshape(piece_blocks, GROUP, value_width)

        centre = cumul[:, GROUP // 2, :]
        q_scaled = q_float * jnp.exp(cumul - centre[:, None, :])
        k_scaled = k_float * jnp.exp(centre[:, None, :] - cumul)
        raw_scores = jnp.einsum("ncd,nsd->ncs", q_scaled, k_scaled, precision=HIGHEST)
        allowed = causal[None] & (seg_blocks[:, :, None] == seg_blocks[:, None, :])
        scores = jnp.where(allowed, raw_scores, 0.0)
        intra = jnp.einsum("ncs,nsv->ncv", scores, v_float, precision=HIGHEST)

        block_totals = cumul[:, -1, :]
        same_last = (seg_blocks == seg_blocks[:, -1:]).astype(jnp.float32)
        k_decayed = k_float * jnp.exp(block_totals[:, None, :] - cumul) * same_last[:, :, None]
        chunk_states = jnp.einsum("ncd,ncv->ndv", k_decayed, v_float, precision=HIGHEST)
        chunk_decay = jnp.exp(block_totals) * live_blocks[:, -1:]
        parts.append(
            (query, outgate, q_float, cumul, live_blocks, intra, chunk_states, chunk_decay, block_totals)
        )

    entering = jnp.zeros((key_width, value_width), jnp.float32)
    local_outs = []
    for p in range(PIECES):
        query, outgate, q_float, cumul, live_blocks, intra, chunk_states, chunk_decay, _ = parts[p]
        states = []
        for n in range(piece_blocks):
            states.append(entering)
            entering = chunk_decay[n][:, None] * entering + chunk_states[n]
        inter = (
            jnp.einsum("ncd,ndv->ncv", q_float * jnp.exp(cumul), jnp.stack(states), precision=HIGHEST)
            * live_blocks[:, :, None]
        )
        local_outs.append((intra + inter).reshape(piece_rows, value_width))
    final_state = entering

    block_totals = jnp.concatenate([part[8] for part in parts])
    before = jnp.cumsum(block_totals, axis=0) - block_totals
    cumul = jnp.concatenate([part[3] for part in parts])
    device_cumul = (cumul + before[:, None, :]).reshape(tok_rows, key_width)

    devices = lax.axis_size("req")
    window = min(devices - 1, -(-SEG_MOST // tok_rows))
    first_id = (segment[0] + 1).astype(jnp.float32)
    last_id = (segment[-1] + 1).astype(jnp.float32)
    decay_device = jnp.exp(device_cumul[-1]) * live_device[-1]
    tail = jnp.zeros((2, value_width), jnp.float32)
    tail = tail.at[0, :key_width].set(decay_device).at[1, 0].set(first_id).at[1, 1].set(last_id)
    message = jnp.concatenate([final_state, tail]).astype(jnp.bfloat16)
    got = [shifted(message, "req", j, devices).astype(jnp.float32) for j in range(1, window + 1)]
    state_in = got[-1][:key_width]
    last_far = got[-1][key_width + 1, 1]
    for j in range(window - 1, 0, -1):
        msg = got[j - 1]
        link = (msg[key_width + 1, 0] == last_far).astype(jnp.float32)
        state_in = msg[:key_width] + (link * msg[key_width, :key_width])[:, None] * state_in
        last_far = msg[key_width + 1, 1]
    linked = (first_id == last_far).astype(jnp.float32)
    mask = live_device * linked

    outs = []
    for p in range(PIECES):
        rows = slice(p * piece_rows, (p + 1) * piece_rows)
        query, outgate = parts[p][0], parts[p][1]
        carried = jnp.dot(
            query.astype(jnp.float32) * jnp.exp(device_cumul[rows]), state_in, precision=HIGHEST
        )
        attn = (local_outs[p] + carried * mask[rows][:, None]) * key_width ** (-0.5)
        normed = attn * lax.rsqrt(jnp.mean(attn * attn, axis=-1, keepdims=True) + 1e-05) * norm_gain
        gated = (normed * jax.nn.silu(outgate)).astype(jnp.bfloat16)
        head_term = jnp.dot(gated, w_out, preferred_element_type=jnp.float32)
        outs.append(
            lax.psum_scatter(head_term.astype(jnp.bfloat16), "tensor", scatter_dimension=1, tiled=True)
        )
    return jnp.concatenate(outs, axis=0)


def solution(mesh):
    in_specs = (
        P("req", "tensor"),
        P("req"),
        P(None, "tensor"),
        P(None, "tensor"),
        P(None, "tensor"),
        P(None, "tensor"),
        P(),
        P(None, "tensor"),
        P("tensor"),
        P(),
        P("tensor", None),
    )
    out_specs = P("req", "tensor")
    return jax.shard_map(body, mesh=mesh, in_specs=in_specs, out_specs=out_specs, check_vma=False)
```

```python
import jax
import jax.numpy as jnp
from jax import lax
from jax.sharding import PartitionSpec as P

GROUP = 64
SEG_MOST = 4096
HIGHEST = lax.Precision.HIGHEST
HIGH = lax.Precision.HIGH


def shifted(x, axis, shift, devices):
    pairs = [(i, i + shift) for i in range(devices - shift)]
    return lax.ppermute(x, axis, pairs)


def body(
    hidden_in,
    segment,
    w_query,
    w_key,
    w_value,
    w_outgate,
    w_gate_down,
    w_gate_up,
    gate_bias,
    norm_gain,
    w_out,
):
    tok_rows = hidden_in.shape[0]
    key_width = w_query.shape[1]
    value_width = w_value.shape[1]
    weights = (w_query, w_key, w_value, w_outgate, w_gate_down)
    piece = lax.all_gather(hidden_in, "tensor", axis=1, tiled=True)
    query_sum, key_sum, value_sum, outgate, low = tuple(
        (jnp.dot(piece, weight, preferred_element_type=jnp.float32) for weight in weights)
    )
    query = query_sum.astype(jnp.bfloat16)
    key = key_sum.astype(jnp.bfloat16)
    value = value_sum.astype(jnp.bfloat16)
    pre_gate = jnp.dot(low, w_gate_up.astype(jnp.float32), precision=HIGHEST) + gate_bias
    logdecay = jax.nn.log_sigmoid(pre_gate) / 16.0

    blocks = tok_rows // GROUP
    starts = jnp.concatenate(
        [jnp.zeros((1,), jnp.int32), (segment[1:] != segment[:-1]).astype(jnp.int32)]
    )
    live_device = (jnp.cumsum(starts) == 0).astype(jnp.float32)
    seg_blocks = segment.reshape(blocks, GROUP)
    live_blocks = (jnp.cumsum(starts.reshape(blocks, GROUP), axis=1) == 0).astype(jnp.float32)
    cumul = jnp.cumsum(logdecay.reshape(blocks, GROUP, key_width), axis=1)
    block_totals = cumul[:, -1, :]
    before = jnp.cumsum(block_totals, axis=0) - block_totals
    device_cumul = (cumul + before[:, None, :]).reshape(tok_rows, key_width)

    q_float = query.astype(jnp.float32).reshape(blocks, GROUP, key_width)
    k_float = key.astype(jnp.float32).reshape(blocks, GROUP, key_width)
    v_float = value.astype(jnp.float32).reshape(blocks, GROUP, value_width)

    positions = jnp.arange(GROUP)
    causal = positions[None, :] <= positions[:, None]
    centre = cumul[:, GROUP // 2, :]
    q_scaled = q_float * jnp.exp(cumul - centre[:, None, :])
    k_scaled = k_float * jnp.exp(centre[:, None, :] - cumul)
    raw_scores = jnp.einsum("ncd,nsd->ncs", q_scaled, k_scaled, precision=HIGH)
    allowed = causal[None] & (seg_blocks[:, :, None] == seg_blocks[:, None, :])
    scores = jnp.where(allowed, raw_scores, 0.0)
    intra = jnp.einsum("ncs,nsv->ncv", scores, v_float, precision=HIGH)

    same_last = (seg_blocks == seg_blocks[:, -1:]).astype(jnp.float32)
    k_decayed = k_float * jnp.exp(block_totals[:, None, :] - cumul) * same_last[:, :, None]
    chunk_states = jnp.einsum("ncd,ncv->ndv", k_decayed, v_float, precision=HIGH)
    chunk_decay = jnp.exp(block_totals) * live_blocks[:, -1:]

    entering = [jnp.zeros((key_width, value_width), jnp.float32)]
    for n in range(blocks):
        entering.append(chunk_decay[n][:, None] * entering[-1] + chunk_states[n])
    final_state = entering[-1]
    entering = jnp.stack(entering[:-1])
    inter = (
        jnp.einsum("ncd,ndv->ncv", q_float * jnp.exp(cumul), entering, precision=HIGH)
        * live_blocks[:, :, None]
    )
    local_out = (intra + inter).reshape(tok_rows, value_width)

    devices = lax.axis_size("req")
    window = min(devices - 1, -(-SEG_MOST // tok_rows))
    first_id = (segment[0] + 1).astype(jnp.float32)
    last_id = (segment[-1] + 1).astype(jnp.float32)
    decay_device = jnp.exp(device_cumul[-1]) * live_device[-1]
    tail = jnp.zeros((2, value_width), jnp.float32)
    tail = tail.at[0, :key_width].set(decay_device).at[1, 0].set(first_id).at[1, 1].set(last_id)
    message = jnp.concatenate([final_state, tail]).astype(jnp.bfloat16)
    got = [shifted(message, "req", j, devices).astype(jnp.float32) for j in range(1, window + 1)]
    state_in = got[-1][:key_width]
    last_far = got[-1][key_width + 1, 1]
    for j in range(window - 1, 0, -1):
        msg = got[j - 1]
        link = (msg[key_width + 1, 0] == last_far).astype(jnp.float32)
        state_in = msg[:key_width] + (link * msg[key_width, :key_width])[:, None] * state_in
        last_far = msg[key_width + 1, 1]
    linked = (first_id == last_far).astype(jnp.float32)
    carried = jnp.dot(
        query.astype(jnp.float32) * jnp.exp(device_cumul), state_in, precision=HIGH
    )
    attn = (local_out + carried * (live_device * linked)[:, None]) * key_width ** (-0.5)
    normed = attn * lax.rsqrt(jnp.mean(attn * attn, axis=-1, keepdims=True) + 1e-05) * norm_gain
    gated = (normed * jax.nn.silu(outgate)).astype(jnp.bfloat16)
    head_term = jnp.dot(gated, w_out, preferred_element_type=jnp.float32)
    return lax.psum_scatter(
        head_term.astype(jnp.bfloat16), "tensor", scatter_dimension=1, tiled=True
    )


def solution(mesh):
    in_specs = (
        P("req", "tensor"),
        P("req"),
        P(None, "tensor"),
        P(None, "tensor"),
        P(None, "tensor"),
        P(None, "tensor"),
        P(),
        P(None, "tensor"),
        P("tensor"),
        P(),
        P("tensor", None),
    )
    out_specs = P("req", "tensor")
    return jax.shard_map(body, mesh=mesh, in_specs=in_specs, out_specs=out_specs, check_vma=False)
```

```python
import jax
import jax.numpy as jnp
from jax import lax
from jax.sharding import PartitionSpec as P

GROUP = 64
SEG_MOST = 4096
HIGHEST = lax.Precision.HIGHEST
HIGH = lax.Precision.HIGH


def shifted(x, axis, shift, devices):
    pairs = [(i, i + shift) for i in range(devices - shift)]
    return lax.ppermute(x, axis, pairs)


def ring(x, step):
    size = lax.axis_size("tensor")
    return lax.ppermute(x, "tensor", [(i, (i + step) % size) for i in range(size)])


def gathered_blocks(local):
    half = local.shape[0] // 2
    from_left = ring(local, 1)
    from_right = ring(local, -1)
    far = jnp.concatenate([ring(from_left[:half], 1), ring(from_right[half:], -1)])
    return ((0, local), (-1, from_left), (1, from_right), (2, far))


def block_dot(blocks_in, weight):
    size = lax.axis_size("tensor")
    index = lax.axis_index("tensor")
    width = blocks_in[0][1].shape[1]
    total = None
    for offset, block in blocks_in:
        rows = lax.dynamic_slice_in_dim(weight, ((index + offset) % size) * width, width, 0)
        term = jnp.dot(block, rows, preferred_element_type=jnp.float32)
        total = term if total is None else total + term
    return total


def scattered_sum(gated, w_out):
    size = lax.axis_size("tensor")
    index = lax.axis_index("tensor")
    width = w_out.shape[1] // size

    def term(offset):
        cols = lax.dynamic_slice_in_dim(w_out, ((index + offset) % size) * width, width, 1)
        return jnp.dot(gated, cols, preferred_element_type=jnp.float32).astype(jnp.bfloat16)

    half = gated.shape[0] // 2
    far = term(2)
    far_from_left = ring(far[:half], 1)
    far_from_right = ring(far[half:], -1)
    from_left = ring(term(1), 1)
    from_right = ring(term(-1), -1)
    relayed = jnp.concatenate([ring(far_from_left, 1), ring(far_from_right, -1)])
    total = term(0).astype(jnp.float32) + from_left.astype(jnp.float32)
    total = total + from_right.astype(jnp.float32) + relayed.astype(jnp.float32)
    return total


def body(
    hidden_in,
    segment,
    w_query,
    w_key,
    w_value,
    w_outgate,
    w_gate_down,
    w_gate_up,
    gate_bias,
    norm_gain,
    w_out,
):
    tok_rows = hidden_in.shape[0]
    key_width = w_query.shape[1]
    value_width = w_value.shape[1]
    weights = (w_query, w_key, w_value, w_outgate, w_gate_down)
    blocks_in = gathered_blocks(hidden_in)
    query_sum, key_sum, value_sum, outgate, low = tuple(
        (block_dot(blocks_in, weight) for weight in weights)
    )
    query = query_sum.astype(jnp.bfloat16)
    key = key_sum.astype(jnp.bfloat16)
    value = value_sum.astype(jnp.bfloat16)
    pre_gate = jnp.dot(low, w_gate_up.astype(jnp.float32), precision=HIGHEST) + gate_bias
    logdecay = jax.nn.log_sigmoid(pre_gate) / 16.0

    blocks = tok_rows // GROUP
    starts = jnp.concatenate(
        [jnp.zeros((1,), jnp.int32), (segment[1:] != segment[:-1]).astype(jnp.int32)]
    )
    live_device = (jnp.cumsum(starts) == 0).astype(jnp.float32)
    seg_blocks = segment.reshape(blocks, GROUP)
    live_blocks = (jnp.cumsum(starts.reshape(blocks, GROUP), axis=1) == 0).astype(jnp.float32)
    cumul = jnp.cumsum(logdecay.reshape(blocks, GROUP, key_width), axis=1)
    block_totals = cumul[:, -1, :]
    before = jnp.cumsum(block_totals, axis=0) - block_totals
    device_cumul = (cumul + before[:, None, :]).reshape(tok_rows, key_width)

    q_float = query.astype(jnp.float32).reshape(blocks, GROUP, key_width)
    k_float = key.astype(jnp.float32).reshape(blocks, GROUP, key_width)
    v_float = value.astype(jnp.float32).reshape(blocks, GROUP, value_width)

    positions = jnp.arange(GROUP)
    causal = positions[None, :] <= positions[:, None]
    centre = cumul[:, GROUP // 2, :]
    q_scaled = q_float * jnp.exp(cumul - centre[:, None, :])
    k_scaled = k_float * jnp.exp(centre[:, None, :] - cumul)
    raw_scores = jnp.einsum("ncd,nsd->ncs", q_scaled, k_scaled, precision=HIGH)
    allowed = causal[None] & (seg_blocks[:, :, None] == seg_blocks[:, None, :])
    scores = jnp.where(allowed, raw_scores, 0.0)
    intra = jnp.einsum("ncs,nsv->ncv", scores, v_float, precision=HIGH)

    same_last = (seg_blocks == seg_blocks[:, -1:]).astype(jnp.float32)
    k_decayed = k_float * jnp.exp(block_totals[:, None, :] - cumul) * same_last[:, :, None]
    chunk_states = jnp.einsum("ncd,ncv->ndv", k_decayed, v_float, precision=HIGH)
    chunk_decay = jnp.exp(block_totals) * live_blocks[:, -1:]

    q_decayed = q_float * jnp.exp(cumul)
    entering = jnp.zeros((key_width, value_width), jnp.float32)
    inters = []
    for n in range(blocks):
        inters.append(jnp.dot(q_decayed[n], entering, precision=HIGH))
        entering = chunk_decay[n][:, None] * entering + chunk_states[n]
    final_state = entering
    inter = jnp.stack(inters) * live_blocks[:, :, None]
    local_out = (intra + inter).reshape(tok_rows, value_width)

    devices = lax.axis_size("req")
    window = min(devices - 1, -(-SEG_MOST // tok_rows))
    first_id = (segment[0] + 1).astype(jnp.float32)
    last_id = (segment[-1] + 1).astype(jnp.float32)
    decay_device = jnp.exp(device_cumul[-1]) * live_device[-1]
    tail = jnp.zeros((2, value_width), jnp.float32)
    tail = tail.at[0, :key_width].set(decay_device).at[1, 0].set(first_id).at[1, 1].set(last_id)
    message = jnp.concatenate([final_state, tail]).astype(jnp.bfloat16)
    got = [shifted(message, "req", j, devices).astype(jnp.float32) for j in range(1, window + 1)]
    state_in = got[-1][:key_width]
    last_far = got[-1][key_width + 1, 1]
    for j in range(window - 1, 0, -1):
        msg = got[j - 1]
        link = (msg[key_width + 1, 0] == last_far).astype(jnp.float32)
        state_in = msg[:key_width] + (link * msg[key_width, :key_width])[:, None] * state_in
        last_far = msg[key_width + 1, 1]
    linked = (first_id == last_far).astype(jnp.float32)
    carried = jnp.dot(
        query.astype(jnp.float32) * jnp.exp(device_cumul), state_in, precision=HIGH
    )
    attn = (local_out + carried * (live_device * linked)[:, None]) * key_width ** (-0.5)
    normed = attn * lax.rsqrt(jnp.mean(attn * attn, axis=-1, keepdims=True) + 1e-05) * norm_gain
    gated = (normed * jax.nn.silu(outgate)).astype(jnp.bfloat16)
    return scattered_sum(gated, w_out).astype(jnp.bfloat16)


def solution(mesh):
    in_specs = (
        P("req", "tensor"),
        P("req"),
        P(None, "tensor"),
        P(None, "tensor"),
        P(None, "tensor"),
        P(None, "tensor"),
        P(),
        P(None, "tensor"),
        P("tensor"),
        P(),
        P("tensor", None),
    )
    out_specs = P("req", "tensor")
    return jax.shard_map(body, mesh=mesh, in_specs=in_specs, out_specs=out_specs, check_vma=False)
```

```python
import jax
import jax.numpy as jnp
from jax import lax
from jax.sharding import PartitionSpec as P

GROUP = 64
SEG_MOST = 4096
HIGHEST = lax.Precision.HIGHEST
HIGH = lax.Precision.HIGH


def shifted(x, axis, shift, devices):
    pairs = [(i, i + shift) for i in range(devices - shift)]
    return lax.ppermute(x, axis, pairs)


def ring(x, step):
    size = lax.axis_size("tensor")
    return lax.ppermute(x, "tensor", [(i, (i + step) % size) for i in range(size)])


def gathered(local):
    half = local.shape[0] // 2
    from_left = ring(local, 1)
    from_right = ring(local, -1)
    far = jnp.concatenate([ring(from_left[:half], 1), ring(from_right[half:], -1)])
    return jnp.concatenate([local, from_right, far, from_left], axis=1)


def projected(full, weights):
    size = lax.axis_size("tensor")
    index = lax.axis_index("tensor")
    width = full.shape[1] // size
    joined = jnp.concatenate(weights, axis=1)
    doubled = jnp.concatenate([joined, joined], axis=0)
    rolled = lax.dynamic_slice_in_dim(doubled, index * width, joined.shape[0], 0)
    out = jnp.dot(full, rolled, preferred_element_type=jnp.float32)
    parts, at = [], 0
    for weight in weights:
        parts.append(out[:, at : at + weight.shape[1]])
        at += weight.shape[1]
    return parts


def scattered_sum(gated, w_out):
    size = lax.axis_size("tensor")
    index = lax.axis_index("tensor")
    width = w_out.shape[1] // size
    rows = gated.shape[0]
    half = rows // 2

    def term(offset):
        cols = lax.dynamic_slice_in_dim(w_out, ((index + offset) % size) * width, width, 1)
        return jnp.dot(gated, cols, preferred_element_type=jnp.float32).astype(jnp.bfloat16)

    far = term(2)
    from_left = ring(jnp.concatenate([term(1), far[:half]]), 1)
    from_right = ring(jnp.concatenate([term(-1), far[half:]]), -1)
    relayed = jnp.concatenate([ring(from_left[rows:], 1), ring(from_right[rows:], -1)])
    total = term(0).astype(jnp.float32) + from_left[:rows].astype(jnp.float32)
    total = total + from_right[:rows].astype(jnp.float32) + relayed.astype(jnp.float32)
    return total


def body(
    hidden_in,
    segment,
    w_query,
    w_key,
    w_value,
    w_outgate,
    w_gate_down,
    w_gate_up,
    gate_bias,
    norm_gain,
    w_out,
):
    tok_rows = hidden_in.shape[0]
    key_width = w_query.shape[1]
    value_width = w_value.shape[1]
    weights = (w_query, w_key, w_value, w_outgate, w_gate_down)
    query_sum, key_sum, value_sum, outgate, low = projected(gathered(hidden_in), weights)
    query = query_sum.astype(jnp.bfloat16)
    key = key_sum.astype(jnp.bfloat16)
    value = value_sum.astype(jnp.bfloat16)
    pre_gate = jnp.dot(low, w_gate_up.astype(jnp.float32), precision=HIGHEST) + gate_bias
    logdecay = jax.nn.log_sigmoid(pre_gate) / 16.0

    blocks = tok_rows // GROUP
    starts = jnp.concatenate(
        [jnp.zeros((1,), jnp.int32), (segment[1:] != segment[:-1]).astype(jnp.int32)]
    )
    live_device = (jnp.cumsum(starts) == 0).astype(jnp.float32)
    seg_blocks = segment.reshape(blocks, GROUP)
    live_blocks = (jnp.cumsum(starts.reshape(blocks, GROUP), axis=1) == 0).astype(jnp.float32)
    cumul = jnp.cumsum(logdecay.reshape(blocks, GROUP, key_width), axis=1)
    block_totals = cumul[:, -1, :]
    before = jnp.cumsum(block_totals, axis=0) - block_totals
    device_cumul = (cumul + before[:, None, :]).reshape(tok_rows, key_width)

    q_float = query.astype(jnp.float32).reshape(blocks, GROUP, key_width)
    k_float = key.astype(jnp.float32).reshape(blocks, GROUP, key_width)
    v_float = value.astype(jnp.float32).reshape(blocks, GROUP, value_width)

    positions = jnp.arange(GROUP)
    causal = positions[None, :] <= positions[:, None]
    centre = cumul[:, GROUP // 2, :]
    q_scaled = q_float * jnp.exp(cumul - centre[:, None, :])
    k_scaled = k_float * jnp.exp(centre[:, None, :] - cumul)
    raw_scores = jnp.einsum("ncd,nsd->ncs", q_scaled, k_scaled, precision=HIGH)
    allowed = causal[None] & (seg_blocks[:, :, None] == seg_blocks[:, None, :])
    scores = jnp.where(allowed, raw_scores, 0.0)
    intra = jnp.einsum("ncs,nsv->ncv", scores, v_float, precision=HIGH)

    same_last = (seg_blocks == seg_blocks[:, -1:]).astype(jnp.float32)
    k_decayed = k_float * jnp.exp(block_totals[:, None, :] - cumul) * same_last[:, :, None]
    chunk_states = jnp.einsum("ncd,ncv->ndv", k_decayed, v_float, precision=HIGH)
    chunk_decay = jnp.exp(block_totals) * live_blocks[:, -1:]

    q_decayed = q_float * jnp.exp(cumul)
    entering = jnp.zeros((key_width, value_width), jnp.float32)
    inters = []
    for n in range(blocks):
        inters.append(jnp.dot(q_decayed[n], entering, precision=HIGH))
        entering = chunk_decay[n][:, None] * entering + chunk_states[n]
    final_state = entering
    inter = jnp.stack(inters) * live_blocks[:, :, None]
    local_out = (intra + inter).reshape(tok_rows, value_width)

    devices = lax.axis_size("req")
    window = min(devices - 1, -(-SEG_MOST // tok_rows))
    first_id = (segment[0] + 1).astype(jnp.float32)
    last_id = (segment[-1] + 1).astype(jnp.float32)
    decay_device = jnp.exp(device_cumul[-1]) * live_device[-1]
    tail = jnp.zeros((2, value_width), jnp.float32)
    tail = tail.at[0, :key_width].set(decay_device).at[1, 0].set(first_id).at[1, 1].set(last_id)
    message = jnp.concatenate([final_state, tail]).astype(jnp.bfloat16)
    got = [shifted(message, "req", j, devices).astype(jnp.float32) for j in range(1, window + 1)]
    state_in = got[-1][:key_width]
    last_far = got[-1][key_width + 1, 1]
    for j in range(window - 1, 0, -1):
        msg = got[j - 1]
        link = (msg[key_width + 1, 0] == last_far).astype(jnp.float32)
        state_in = msg[:key_width] + (link * msg[key_width, :key_width])[:, None] * state_in
        last_far = msg[key_width + 1, 1]
    linked = (first_id == last_far).astype(jnp.float32)
    carried = jnp.dot(
        query.astype(jnp.float32) * jnp.exp(device_cumul), state_in, precision=HIGH
    )
    attn = (local_out + carried * (live_device * linked)[:, None]) * key_width ** (-0.5)
    normed = attn * lax.rsqrt(jnp.mean(attn * attn, axis=-1, keepdims=True) + 1e-05) * norm_gain
    gated = (normed * jax.nn.silu(outgate)).astype(jnp.bfloat16)
    return scattered_sum(gated, w_out).astype(jnp.bfloat16)


def solution(mesh):
    in_specs = (
        P("req", "tensor"),
        P("req"),
        P(None, "tensor"),
        P(None, "tensor"),
        P(None, "tensor"),
        P(None, "tensor"),
        P(),
        P(None, "tensor"),
        P("tensor"),
        P(),
        P("tensor", None),
    )
    out_specs = P("req", "tensor")
    return jax.shard_map(body, mesh=mesh, in_specs=in_specs, out_specs=out_specs, check_vma=False)
```

```python
import jax
import jax.numpy as jnp
from jax import lax
from jax.sharding import PartitionSpec as P

GROUP = 64
SEG_MOST = 4096
HIGHEST = lax.Precision.HIGHEST
HIGH = lax.Precision.HIGH


def shifted(x, axis, shift, devices):
    pairs = [(i, i + shift) for i in range(devices - shift)]
    return lax.ppermute(x, axis, pairs)


def ring(x, step):
    size = lax.axis_size("tensor")
    return lax.ppermute(x, "tensor", [(i, (i + step) % size) for i in range(size)])


def gathered(local):
    half = local.shape[0] // 2
    from_left = ring(local, 1)
    from_right = ring(local, -1)
    far = jnp.concatenate([ring(from_left[:half], 1), ring(from_right[half:], -1)])
    return jnp.concatenate([local, from_right, far, from_left], axis=1)


def projected(full, weights):
    size = lax.axis_size("tensor")
    index = lax.axis_index("tensor")
    width = full.shape[1] // size
    joined = jnp.concatenate(weights, axis=1)
    doubled = jnp.concatenate([joined, joined], axis=0)
    rolled = lax.dynamic_slice_in_dim(doubled, index * width, joined.shape[0], 0)
    out = jnp.dot(full, rolled, preferred_element_type=jnp.float32)
    parts, at = [], 0
    for weight in weights:
        parts.append(out[:, at : at + weight.shape[1]])
        at += weight.shape[1]
    return parts


def scattered_sum(gated, w_out):
    size = lax.axis_size("tensor")
    index = lax.axis_index("tensor")
    width = w_out.shape[1] // size
    rows = gated.shape[0]
    half = rows // 2

    def term(offset):
        cols = lax.dynamic_slice_in_dim(w_out, ((index + offset) % size) * width, width, 1)
        return jnp.dot(gated, cols, preferred_element_type=jnp.float32).astype(jnp.bfloat16)

    far = term(2)
    far_from_left = ring(far[:half], 1)
    far_from_right = ring(far[half:], -1)
    from_left = ring(term(1), 1)
    from_right = ring(term(-1), -1)
    relayed = jnp.concatenate([ring(far_from_left, 1), ring(far_from_right, -1)])
    total = term(0).astype(jnp.float32) + from_left.astype(jnp.float32)
    total = total + from_right.astype(jnp.float32) + relayed.astype(jnp.float32)
    return total


def body(
    hidden_in,
    segment,
    w_query,
    w_key,
    w_value,
    w_outgate,
    w_gate_down,
    w_gate_up,
    gate_bias,
    norm_gain,
    w_out,
):
    tok_rows = hidden_in.shape[0]
    key_width = w_query.shape[1]
    value_width = w_value.shape[1]
    weights = (w_query, w_key, w_value, w_outgate, w_gate_down)
    query_sum, key_sum, value_sum, outgate, low = projected(gathered(hidden_in), weights)
    query = query_sum.astype(jnp.bfloat16)
    key = key_sum.astype(jnp.bfloat16)
    value = value_sum.astype(jnp.bfloat16)
    pre_gate = jnp.dot(low, w_gate_up.astype(jnp.float32), precision=HIGHEST) + gate_bias
    logdecay = jax.nn.log_sigmoid(pre_gate) / 16.0

    blocks = tok_rows // GROUP
    starts = jnp.concatenate(
        [jnp.zeros((1,), jnp.int32), (segment[1:] != segment[:-1]).astype(jnp.int32)]
    )
    live_device = (jnp.cumsum(starts) == 0).astype(jnp.float32)
    seg_blocks = segment.reshape(blocks, GROUP)
    live_blocks = (jnp.cumsum(starts.reshape(blocks, GROUP), axis=1) == 0).astype(jnp.float32)
    cumul = jnp.cumsum(logdecay.reshape(blocks, GROUP, key_width), axis=1)
    block_totals = cumul[:, -1, :]
    before = jnp.cumsum(block_totals, axis=0) - block_totals
    device_cumul = (cumul + before[:, None, :]).reshape(tok_rows, key_width)

    q_float = query.astype(jnp.float32).reshape(blocks, GROUP, key_width)
    k_float = key.astype(jnp.float32).reshape(blocks, GROUP, key_width)
    v_float = value.astype(jnp.float32).reshape(blocks, GROUP, value_width)

    positions = jnp.arange(GROUP)
    causal = positions[None, :] <= positions[:, None]
    centre = cumul[:, GROUP // 2, :]
    q_scaled = q_float * jnp.exp(cumul - centre[:, None, :])
    k_scaled = k_float * jnp.exp(centre[:, None, :] - cumul)
    raw_scores = jnp.einsum("ncd,nsd->ncs", q_scaled, k_scaled, precision=HIGH)
    allowed = causal[None] & (seg_blocks[:, :, None] == seg_blocks[:, None, :])
    scores = jnp.where(allowed, raw_scores, 0.0)
    intra = jnp.einsum("ncs,nsv->ncv", scores, v_float, precision=HIGH)

    same_last = (seg_blocks == seg_blocks[:, -1:]).astype(jnp.float32)
    k_decayed = k_float * jnp.exp(block_totals[:, None, :] - cumul) * same_last[:, :, None]
    chunk_states = jnp.einsum("ncd,ncv->ndv", k_decayed, v_float, precision=HIGH)
    chunk_decay = jnp.exp(block_totals) * live_blocks[:, -1:]

    q_decayed = q_float * jnp.exp(cumul)
    entering = jnp.zeros((key_width, value_width), jnp.float32)
    inters = []
    for n in range(blocks):
        inters.append(jnp.dot(q_decayed[n], entering, precision=HIGH))
        entering = chunk_decay[n][:, None] * entering + chunk_states[n]
    final_state = entering
    inter = jnp.stack(inters) * live_blocks[:, :, None]
    local_out = (intra + inter).reshape(tok_rows, value_width)

    devices = lax.axis_size("req")
    window = min(devices - 1, -(-SEG_MOST // tok_rows))
    first_id = (segment[0] + 1).astype(jnp.float32)
    last_id = (segment[-1] + 1).astype(jnp.float32)
    decay_device = jnp.exp(device_cumul[-1]) * live_device[-1]
    tail = jnp.zeros((2, value_width), jnp.float32)
    tail = tail.at[0, :key_width].set(decay_device).at[1, 0].set(first_id).at[1, 1].set(last_id)
    message = jnp.concatenate([final_state, tail]).astype(jnp.bfloat16)
    got = [shifted(message, "req", j, devices).astype(jnp.float32) for j in range(1, window + 1)]
    state_in = got[-1][:key_width]
    last_far = got[-1][key_width + 1, 1]
    for j in range(window - 1, 0, -1):
        msg = got[j - 1]
        link = (msg[key_width + 1, 0] == last_far).astype(jnp.float32)
        state_in = msg[:key_width] + (link * msg[key_width, :key_width])[:, None] * state_in
        last_far = msg[key_width + 1, 1]
    linked = (first_id == last_far).astype(jnp.float32)
    carried = jnp.dot(
        query.astype(jnp.float32) * jnp.exp(device_cumul), state_in, precision=HIGH
    )
    attn = (local_out + carried * (live_device * linked)[:, None]) * key_width ** (-0.5)
    normed = attn * lax.rsqrt(jnp.mean(attn * attn, axis=-1, keepdims=True) + 1e-05) * norm_gain
    gated = (normed * jax.nn.silu(outgate)).astype(jnp.bfloat16)
    return scattered_sum(gated, w_out).astype(jnp.bfloat16)


def solution(mesh):
    in_specs = (
        P("req", "tensor"),
        P("req"),
        P(None, "tensor"),
        P(None, "tensor"),
        P(None, "tensor"),
        P(None, "tensor"),
        P(),
        P(None, "tensor"),
        P("tensor"),
        P(),
        P("tensor", None),
    )
    out_specs = P("req", "tensor")
    return jax.shard_map(body, mesh=mesh, in_specs=in_specs, out_specs=out_specs, check_vma=False)
```

```python
import jax
import jax.numpy as jnp
from jax import lax
from jax.sharding import PartitionSpec as P

GROUP = 64
SEG_MOST = 4096
HIGHEST = lax.Precision.HIGHEST
HIGH = lax.Precision.HIGH


def shifted(x, axis, shift, devices):
    pairs = [(i, i + shift) for i in range(devices - shift)]
    return lax.ppermute(x, axis, pairs)


def ring(x, step):
    size = lax.axis_size("tensor")
    return lax.ppermute(x, "tensor", [(i, (i + step) % size) for i in range(size)])


def gathered(local):
    half = local.shape[0] // 2
    left_a = ring(local[:half], 1)
    right_a = ring(local[half:], -1)
    left_a, right_a, rest = lax.optimization_barrier((left_a, right_a, local))
    left_b = ring(rest[half:], 1)
    right_b = ring(rest[:half], -1)
    far = jnp.concatenate([ring(left_a, 1), ring(right_a, -1)])
    from_left = jnp.concatenate([left_a, left_b])
    from_right = jnp.concatenate([right_b, right_a])
    return jnp.concatenate([local, from_right, far, from_left], axis=1)


def projected(full, weights):
    size = lax.axis_size("tensor")
    index = lax.axis_index("tensor")
    width = full.shape[1] // size
    joined = jnp.concatenate(weights, axis=1)
    doubled = jnp.concatenate([joined, joined], axis=0)
    rolled = lax.dynamic_slice_in_dim(doubled, index * width, joined.shape[0], 0)
    out = jnp.dot(full, rolled, preferred_element_type=jnp.float32)
    parts, at = [], 0
    for weight in weights:
        parts.append(out[:, at : at + weight.shape[1]])
        at += weight.shape[1]
    return parts


def scattered_sum(gated, w_out):
    size = lax.axis_size("tensor")
    index = lax.axis_index("tensor")
    width = w_out.shape[1] // size
    rows = gated.shape[0]
    half = rows // 2

    def term(offset):
        cols = lax.dynamic_slice_in_dim(w_out, ((index + offset) % size) * width, width, 1)
        return jnp.dot(gated, cols, preferred_element_type=jnp.float32).astype(jnp.bfloat16)

    far = term(2)
    far_from_left = ring(far[:half], 1)
    far_from_right = ring(far[half:], -1)
    near_right, near_left = term(1), term(-1)
    far_from_left, far_from_right, near_right, near_left = lax.optimization_barrier(
        (far_from_left, far_from_right, near_right, near_left)
    )
    from_left = ring(near_right, 1)
    from_right = ring(near_left, -1)
    relayed = jnp.concatenate([ring(far_from_left, 1), ring(far_from_right, -1)])
    total = term(0).astype(jnp.float32) + from_left.astype(jnp.float32)
    total = total + from_right.astype(jnp.float32) + relayed.astype(jnp.float32)
    return total


def body(
    hidden_in,
    segment,
    w_query,
    w_key,
    w_value,
    w_outgate,
    w_gate_down,
    w_gate_up,
    gate_bias,
    norm_gain,
    w_out,
):
    tok_rows = hidden_in.shape[0]
    key_width = w_query.shape[1]
    value_width = w_value.shape[1]
    weights = (w_query, w_key, w_value, w_outgate, w_gate_down)
    query_sum, key_sum, value_sum, outgate, low = projected(gathered(hidden_in), weights)
    query = query_sum.astype(jnp.bfloat16)
    key = key_sum.astype(jnp.bfloat16)
    value = value_sum.astype(jnp.bfloat16)
    pre_gate = jnp.dot(low, w_gate_up.astype(jnp.float32), precision=HIGHEST) + gate_bias
    logdecay = jax.nn.log_sigmoid(pre_gate) / 16.0

    blocks = tok_rows // GROUP
    starts = jnp.concatenate(
        [jnp.zeros((1,), jnp.int32), (segment[1:] != segment[:-1]).astype(jnp.int32)]
    )
    live_device = (jnp.cumsum(starts) == 0).astype(jnp.float32)
    seg_blocks = segment.reshape(blocks, GROUP)
    live_blocks = (jnp.cumsum(starts.reshape(blocks, GROUP), axis=1) == 0).astype(jnp.float32)
    cumul = jnp.cumsum(logdecay.reshape(blocks, GROUP, key_width), axis=1)
    block_totals = cumul[:, -1, :]
    before = jnp.cumsum(block_totals, axis=0) - block_totals
    device_cumul = (cumul + before[:, None, :]).reshape(tok_rows, key_width)

    q_float = query.astype(jnp.float32).reshape(blocks, GROUP, key_width)
    k_float = key.astype(jnp.float32).reshape(blocks, GROUP, key_width)
    v_float = value.astype(jnp.float32).reshape(blocks, GROUP, value_width)

    positions = jnp.arange(GROUP)
    causal = positions[None, :] <= positions[:, None]
    centre = cumul[:, GROUP // 2, :]
    q_scaled = q_float * jnp.exp(cumul - centre[:, None, :])
    k_scaled = k_float * jnp.exp(centre[:, None, :] - cumul)
    raw_scores = jnp.einsum("ncd,nsd->ncs", q_scaled, k_scaled, precision=HIGH)
    allowed = causal[None] & (seg_blocks[:, :, None] == seg_blocks[:, None, :])
    scores = jnp.where(allowed, raw_scores, 0.0)
    intra = jnp.einsum("ncs,nsv->ncv", scores, v_float, precision=HIGH)

    same_last = (seg_blocks == seg_blocks[:, -1:]).astype(jnp.float32)
    k_decayed = k_float * jnp.exp(block_totals[:, None, :] - cumul) * same_last[:, :, None]
    chunk_states = jnp.einsum("ncd,ncv->ndv", k_decayed, v_float, precision=HIGH)
    chunk_decay = jnp.exp(block_totals) * live_blocks[:, -1:]

    q_decayed = q_float * jnp.exp(cumul)
    entering = jnp.zeros((key_width, value_width), jnp.float32)
    inters = []
    for n in range(blocks):
        inters.append(jnp.dot(q_decayed[n], entering, precision=HIGH))
        entering = chunk_decay[n][:, None] * entering + chunk_states[n]
    final_state = entering
    inter = jnp.stack(inters) * live_blocks[:, :, None]
    local_out = (intra + inter).reshape(tok_rows, value_width)

    devices = lax.axis_size("req")
    window = min(devices - 1, -(-SEG_MOST // tok_rows))
    first_id = (segment[0] + 1).astype(jnp.float32)
    last_id = (segment[-1] + 1).astype(jnp.float32)
    decay_device = jnp.exp(device_cumul[-1]) * live_device[-1]
    tail = jnp.zeros((2, value_width), jnp.float32)
    tail = tail.at[0, :key_width].set(decay_device).at[1, 0].set(first_id).at[1, 1].set(last_id)
    message = jnp.concatenate([final_state, tail]).astype(jnp.bfloat16)
    got = [shifted(message, "req", j, devices).astype(jnp.float32) for j in range(1, window + 1)]
    state_in = got[-1][:key_width]
    last_far = got[-1][key_width + 1, 1]
    for j in range(window - 1, 0, -1):
        msg = got[j - 1]
        link = (msg[key_width + 1, 0] == last_far).astype(jnp.float32)
        state_in = msg[:key_width] + (link * msg[key_width, :key_width])[:, None] * state_in
        last_far = msg[key_width + 1, 1]
    linked = (first_id == last_far).astype(jnp.float32)
    carried = jnp.dot(
        query.astype(jnp.float32) * jnp.exp(device_cumul), state_in, precision=HIGH
    )
    attn = (local_out + carried * (live_device * linked)[:, None]) * key_width ** (-0.5)
    normed = attn * lax.rsqrt(jnp.mean(attn * attn, axis=-1, keepdims=True) + 1e-05) * norm_gain
    gated = (normed * jax.nn.silu(outgate)).astype(jnp.bfloat16)
    return scattered_sum(gated, w_out).astype(jnp.bfloat16)


def solution(mesh):
    in_specs = (
        P("req", "tensor"),
        P("req"),
        P(None, "tensor"),
        P(None, "tensor"),
        P(None, "tensor"),
        P(None, "tensor"),
        P(),
        P(None, "tensor"),
        P("tensor"),
        P(),
        P("tensor", None),
    )
    out_specs = P("req", "tensor")
    return jax.shard_map(body, mesh=mesh, in_specs=in_specs, out_specs=out_specs, check_vma=False)
```

```python
import jax
import jax.numpy as jnp
from jax import lax
from jax.sharding import PartitionSpec as P

GROUP = 64
SEG_MOST = 4096
HIGHEST = lax.Precision.HIGHEST
HIGH = lax.Precision.HIGH


def shifted(x, axis, shift, devices):
    pairs = [(i, i + shift) for i in range(devices - shift)]
    return lax.ppermute(x, axis, pairs)


def ring(x, step):
    size = lax.axis_size("tensor")
    return lax.ppermute(x, "tensor", [(i, (i + step) % size) for i in range(size)])


def gathered(local):
    half = local.shape[0] // 2
    left_a = ring(local[:half], 1)
    right_a = ring(local[half:], -1)
    left_a, right_a, rest = lax.optimization_barrier((left_a, right_a, local))
    left_b = ring(rest[half:], 1)
    right_b = ring(rest[:half], -1)
    far = jnp.concatenate([ring(left_a, 1), ring(right_a, -1)])
    from_left = jnp.concatenate([left_a, left_b])
    from_right = jnp.concatenate([right_b, right_a])
    return jnp.concatenate([local, from_right, from_left], axis=1), far


def projected(near, far, weights):
    size = lax.axis_size("tensor")
    index = lax.axis_index("tensor")
    width = far.shape[1]
    joined = jnp.concatenate(weights, axis=1)

    def rows(offset):
        return lax.dynamic_slice_in_dim(joined, ((index + offset) % size) * width, width, 0)

    near_rows = jnp.concatenate([rows(0), rows(1), rows(size - 1)])
    out = jnp.dot(near, near_rows, preferred_element_type=jnp.float32)
    out = out + jnp.dot(far, rows(2), preferred_element_type=jnp.float32)
    parts, at = [], 0
    for weight in weights:
        parts.append(out[:, at : at + weight.shape[1]])
        at += weight.shape[1]
    return parts


def scattered_sum(gated, w_out):
    size = lax.axis_size("tensor")
    index = lax.axis_index("tensor")
    width = w_out.shape[1] // size
    rows = gated.shape[0]
    half = rows // 2

    def term(offset):
        cols = lax.dynamic_slice_in_dim(w_out, ((index + offset) % size) * width, width, 1)
        return jnp.dot(gated, cols, preferred_element_type=jnp.float32).astype(jnp.bfloat16)

    far = term(2)
    far_from_left = ring(far[:half], 1)
    far_from_right = ring(far[half:], -1)
    from_left = ring(term(1), 1)
    from_right = ring(term(-1), -1)
    relayed = jnp.concatenate([ring(far_from_left, 1), ring(far_from_right, -1)])
    total = term(0).astype(jnp.float32) + from_left.astype(jnp.float32)
    total = total + from_right.astype(jnp.float32) + relayed.astype(jnp.float32)
    return total


def body(
    hidden_in,
    segment,
    w_query,
    w_key,
    w_value,
    w_outgate,
    w_gate_down,
    w_gate_up,
    gate_bias,
    norm_gain,
    w_out,
):
    tok_rows = hidden_in.shape[0]
    key_width = w_query.shape[1]
    value_width = w_value.shape[1]
    weights = (w_query, w_key, w_value, w_outgate, w_gate_down)
    query_sum, key_sum, value_sum, outgate, low = projected(*gathered(hidden_in), weights)
    query = query_sum.astype(jnp.bfloat16)
    key = key_sum.astype(jnp.bfloat16)
    value = value_sum.astype(jnp.bfloat16)
    pre_gate = jnp.dot(low, w_gate_up.astype(jnp.float32), precision=HIGHEST) + gate_bias
    logdecay = jax.nn.log_sigmoid(pre_gate) / 16.0

    blocks = tok_rows // GROUP
    starts = jnp.concatenate(
        [jnp.zeros((1,), jnp.int32), (segment[1:] != segment[:-1]).astype(jnp.int32)]
    )
    live_device = (jnp.cumsum(starts) == 0).astype(jnp.float32)
    seg_blocks = segment.reshape(blocks, GROUP)
    live_blocks = (jnp.cumsum(starts.reshape(blocks, GROUP), axis=1) == 0).astype(jnp.float32)
    cumul = jnp.cumsum(logdecay.reshape(blocks, GROUP, key_width), axis=1)
    block_totals = cumul[:, -1, :]
    before = jnp.cumsum(block_totals, axis=0) - block_totals
    device_cumul = (cumul + before[:, None, :]).reshape(tok_rows, key_width)

    q_float = query.astype(jnp.float32).reshape(blocks, GROUP, key_width)
    k_float = key.astype(jnp.float32).reshape(blocks, GROUP, key_width)
    v_float = value.astype(jnp.float32).reshape(blocks, GROUP, value_width)

    positions = jnp.arange(GROUP)
    causal = positions[None, :] <= positions[:, None]
    centre = cumul[:, GROUP // 2, :]
    q_scaled = q_float * jnp.exp(cumul - centre[:, None, :])
    k_scaled = k_float * jnp.exp(centre[:, None, :] - cumul)
    raw_scores = jnp.einsum("ncd,nsd->ncs", q_scaled, k_scaled, precision=HIGH)
    allowed = causal[None] & (seg_blocks[:, :, None] == seg_blocks[:, None, :])
    scores = jnp.where(allowed, raw_scores, 0.0)
    intra = jnp.einsum("ncs,nsv->ncv", scores, v_float, precision=HIGH)

    same_last = (seg_blocks == seg_blocks[:, -1:]).astype(jnp.float32)
    k_decayed = k_float * jnp.exp(block_totals[:, None, :] - cumul) * same_last[:, :, None]
    chunk_states = jnp.einsum("ncd,ncv->ndv", k_decayed, v_float, precision=HIGH)
    chunk_decay = jnp.exp(block_totals) * live_blocks[:, -1:]

    q_decayed = q_float * jnp.exp(cumul)
    entering = jnp.zeros((key_width, value_width), jnp.float32)
    inters = []
    for n in range(blocks):
        inters.append(jnp.dot(q_decayed[n], entering, precision=HIGH))
        entering = chunk_decay[n][:, None] * entering + chunk_states[n]
    final_state = entering
    inter = jnp.stack(inters) * live_blocks[:, :, None]
    local_out = (intra + inter).reshape(tok_rows, value_width)

    devices = lax.axis_size("req")
    window = min(devices - 1, -(-SEG_MOST // tok_rows))
    first_id = (segment[0] + 1).astype(jnp.float32)
    last_id = (segment[-1] + 1).astype(jnp.float32)
    decay_device = jnp.exp(device_cumul[-1]) * live_device[-1]
    tail = jnp.zeros((2, value_width), jnp.float32)
    tail = tail.at[0, :key_width].set(decay_device).at[1, 0].set(first_id).at[1, 1].set(last_id)
    message = jnp.concatenate([final_state, tail]).astype(jnp.bfloat16)
    got = [shifted(message, "req", j, devices).astype(jnp.float32) for j in range(1, window + 1)]
    state_in = got[-1][:key_width]
    last_far = got[-1][key_width + 1, 1]
    for j in range(window - 1, 0, -1):
        msg = got[j - 1]
        link = (msg[key_width + 1, 0] == last_far).astype(jnp.float32)
        state_in = msg[:key_width] + (link * msg[key_width, :key_width])[:, None] * state_in
        last_far = msg[key_width + 1, 1]
    linked = (first_id == last_far).astype(jnp.float32)
    carried = jnp.dot(
        query.astype(jnp.float32) * jnp.exp(device_cumul), state_in, precision=HIGH
    )
    attn = (local_out + carried * (live_device * linked)[:, None]) * key_width ** (-0.5)
    normed = attn * lax.rsqrt(jnp.mean(attn * attn, axis=-1, keepdims=True) + 1e-05) * norm_gain
    gated = (normed * jax.nn.silu(outgate)).astype(jnp.bfloat16)
    return scattered_sum(gated, w_out).astype(jnp.bfloat16)


def solution(mesh):
    in_specs = (
        P("req", "tensor"),
        P("req"),
        P(None, "tensor"),
        P(None, "tensor"),
        P(None, "tensor"),
        P(None, "tensor"),
        P(),
        P(None, "tensor"),
        P("tensor"),
        P(),
        P("tensor", None),
    )
    out_specs = P("req", "tensor")
    return jax.shard_map(body, mesh=mesh, in_specs=in_specs, out_specs=out_specs, check_vma=False)
```

```python
import jax
import jax.numpy as jnp
from jax import lax
from jax.sharding import PartitionSpec as P

GROUP = 64
SEG_MOST = 4096
HIGHEST = lax.Precision.HIGHEST
HIGH = lax.Precision.HIGH


def shifted(x, axis, shift, devices):
    pairs = [(i, i + shift) for i in range(devices - shift)]
    return lax.ppermute(x, axis, pairs)


def ring(x, step):
    size = lax.axis_size("tensor")
    return lax.ppermute(x, "tensor", [(i, (i + step) % size) for i in range(size)])


def gathered(local):
    half = local.shape[0] // 2
    left_a = ring(local[:half], 1)
    right_a = ring(local[half:], -1)
    left_a, right_a, rest = lax.optimization_barrier((left_a, right_a, local))
    left_b = ring(rest[half:], 1)
    right_b = ring(rest[:half], -1)
    far = jnp.concatenate([ring(left_a, 1), ring(right_a, -1)])
    from_left = jnp.concatenate([left_a, left_b])
    from_right = jnp.concatenate([right_b, right_a])
    return jnp.concatenate([local, from_right, from_left], axis=1), far


def projected(near, far, weights):
    size = lax.axis_size("tensor")
    index = lax.axis_index("tensor")
    width = far.shape[1]
    parts = []
    for weight in weights:

        def rows(offset):
            return lax.dynamic_slice_in_dim(weight, ((index + offset) % size) * width, width, 0)

        near_rows = jnp.concatenate([rows(0), rows(1), rows(size - 1)])
        out = jnp.dot(near, near_rows, preferred_element_type=jnp.float32)
        parts.append(out + jnp.dot(far, rows(2), preferred_element_type=jnp.float32))
    return parts


def scattered_sum(gated, w_out):
    size = lax.axis_size("tensor")
    index = lax.axis_index("tensor")
    width = w_out.shape[1] // size
    rows = gated.shape[0]
    half = rows // 2

    def term(offset):
        cols = lax.dynamic_slice_in_dim(w_out, ((index + offset) % size) * width, width, 1)
        return jnp.dot(gated, cols, preferred_element_type=jnp.float32).astype(jnp.bfloat16)

    far = term(2)
    far_from_left = ring(far[:half], 1)
    far_from_right = ring(far[half:], -1)
    from_left = ring(term(1), 1)
    from_right = ring(term(-1), -1)
    relayed = jnp.concatenate([ring(far_from_left, 1), ring(far_from_right, -1)])
    total = term(0).astype(jnp.float32) + from_left.astype(jnp.float32)
    total = total + from_right.astype(jnp.float32) + relayed.astype(jnp.float32)
    return total


def body(
    hidden_in,
    segment,
    w_query,
    w_key,
    w_value,
    w_outgate,
    w_gate_down,
    w_gate_up,
    gate_bias,
    norm_gain,
    w_out,
):
    tok_rows = hidden_in.shape[0]
    key_width = w_query.shape[1]
    value_width = w_value.shape[1]
    weights = (w_query, w_key, w_value, w_outgate, w_gate_down)
    query_sum, key_sum, value_sum, outgate, low = projected(*gathered(hidden_in), weights)
    query = query_sum.astype(jnp.bfloat16)
    key = key_sum.astype(jnp.bfloat16)
    value = value_sum.astype(jnp.bfloat16)
    pre_gate = jnp.dot(low, w_gate_up.astype(jnp.float32), precision=HIGHEST) + gate_bias
    logdecay = jax.nn.log_sigmoid(pre_gate) / 16.0

    blocks = tok_rows // GROUP
    starts = jnp.concatenate(
        [jnp.zeros((1,), jnp.int32), (segment[1:] != segment[:-1]).astype(jnp.int32)]
    )
    live_device = (jnp.cumsum(starts) == 0).astype(jnp.float32)
    seg_blocks = segment.reshape(blocks, GROUP)
    live_blocks = (jnp.cumsum(starts.reshape(blocks, GROUP), axis=1) == 0).astype(jnp.float32)
    cumul = jnp.cumsum(logdecay.reshape(blocks, GROUP, key_width), axis=1)
    block_totals = cumul[:, -1, :]
    before = jnp.cumsum(block_totals, axis=0) - block_totals
    device_cumul = (cumul + before[:, None, :]).reshape(tok_rows, key_width)

    q_float = query.astype(jnp.float32).reshape(blocks, GROUP, key_width)
    k_float = key.astype(jnp.float32).reshape(blocks, GROUP, key_width)
    v_float = value.astype(jnp.float32).reshape(blocks, GROUP, value_width)

    positions = jnp.arange(GROUP)
    causal = positions[None, :] <= positions[:, None]
    centre = cumul[:, GROUP // 2, :]
    q_scaled = q_float * jnp.exp(cumul - centre[:, None, :])
    k_scaled = k_float * jnp.exp(centre[:, None, :] - cumul)
    raw_scores = jnp.einsum("ncd,nsd->ncs", q_scaled, k_scaled, precision=HIGH)
    allowed = causal[None] & (seg_blocks[:, :, None] == seg_blocks[:, None, :])
    scores = jnp.where(allowed, raw_scores, 0.0)
    intra = jnp.einsum("ncs,nsv->ncv", scores, v_float, precision=HIGH)

    same_last = (seg_blocks == seg_blocks[:, -1:]).astype(jnp.float32)
    k_decayed = k_float * jnp.exp(block_totals[:, None, :] - cumul) * same_last[:, :, None]
    chunk_states = jnp.einsum("ncd,ncv->ndv", k_decayed, v_float, precision=HIGH)
    chunk_decay = jnp.exp(block_totals) * live_blocks[:, -1:]

    q_decayed = q_float * jnp.exp(cumul)
    entering = jnp.zeros((key_width, value_width), jnp.float32)
    inters = []
    for n in range(blocks):
        inters.append(jnp.dot(q_decayed[n], entering, precision=HIGH))
        entering = chunk_decay[n][:, None] * entering + chunk_states[n]
    final_state = entering
    inter = jnp.stack(inters) * live_blocks[:, :, None]
    local_out = (intra + inter).reshape(tok_rows, value_width)

    devices = lax.axis_size("req")
    window = min(devices - 1, -(-SEG_MOST // tok_rows))
    first_id = (segment[0] + 1).astype(jnp.float32)
    last_id = (segment[-1] + 1).astype(jnp.float32)
    decay_device = jnp.exp(device_cumul[-1]) * live_device[-1]
    tail = jnp.zeros((2, value_width), jnp.float32)
    tail = tail.at[0, :key_width].set(decay_device).at[1, 0].set(first_id).at[1, 1].set(last_id)
    message = jnp.concatenate([final_state, tail]).astype(jnp.bfloat16)
    got = [shifted(message, "req", j, devices).astype(jnp.float32) for j in range(1, window + 1)]
    state_in = got[-1][:key_width]
    last_far = got[-1][key_width + 1, 1]
    for j in range(window - 1, 0, -1):
        msg = got[j - 1]
        link = (msg[key_width + 1, 0] == last_far).astype(jnp.float32)
        state_in = msg[:key_width] + (link * msg[key_width, :key_width])[:, None] * state_in
        last_far = msg[key_width + 1, 1]
    linked = (first_id == last_far).astype(jnp.float32)
    carried = jnp.dot(
        query.astype(jnp.float32) * jnp.exp(device_cumul), state_in, precision=HIGH
    )
    attn = (local_out + carried * (live_device * linked)[:, None]) * key_width ** (-0.5)
    normed = attn * lax.rsqrt(jnp.mean(attn * attn, axis=-1, keepdims=True) + 1e-05) * norm_gain
    gated = (normed * jax.nn.silu(outgate)).astype(jnp.bfloat16)
    return scattered_sum(gated, w_out).astype(jnp.bfloat16)


def solution(mesh):
    in_specs = (
        P("req", "tensor"),
        P("req"),
        P(None, "tensor"),
        P(None, "tensor"),
        P(None, "tensor"),
        P(None, "tensor"),
        P(),
        P(None, "tensor"),
        P("tensor"),
        P(),
        P("tensor", None),
    )
    out_specs = P("req", "tensor")
    return jax.shard_map(body, mesh=mesh, in_specs=in_specs, out_specs=out_specs, check_vma=False)
```

```python
import jax
import jax.numpy as jnp
from jax import lax
from jax.sharding import PartitionSpec as P

GROUP = 64
SEG_MOST = 4096
HIGHEST = lax.Precision.HIGHEST
HIGH = lax.Precision.HIGH


def shifted(x, axis, shift, devices):
    pairs = [(i, i + shift) for i in range(devices - shift)]
    return lax.ppermute(x, axis, pairs)


def ring(x, step):
    size = lax.axis_size("tensor")
    return lax.ppermute(x, "tensor", [(i, (i + step) % size) for i in range(size)])


def gathered(local):
    half = local.shape[0] // 2
    left_a = ring(local[:half], 1)
    right_a = ring(local[half:], -1)
    left_a, right_a, rest = lax.optimization_barrier((left_a, right_a, local))
    left_b = ring(rest[half:], 1)
    right_b = ring(rest[:half], -1)
    far = jnp.concatenate([ring(left_a, 1), ring(right_a, -1)])
    from_left = jnp.concatenate([left_a, left_b])
    from_right = jnp.concatenate([right_b, right_a])
    return jnp.concatenate([local, from_right, from_left], axis=1), far


def projected(near, far, weights):
    size = lax.axis_size("tensor")
    index = lax.axis_index("tensor")
    width = far.shape[1]
    parts = []
    for weight in weights:

        def rows(offset):
            return lax.dynamic_slice_in_dim(weight, ((index + offset) % size) * width, width, 0)

        near_rows = jnp.concatenate([rows(0), rows(1), rows(size - 1)])
        out = jnp.dot(near, near_rows, preferred_element_type=jnp.float32)
        parts.append(out + jnp.dot(far, rows(2), preferred_element_type=jnp.float32))
    return parts


def scattered_sum(gated, w_out):
    size = lax.axis_size("tensor")
    index = lax.axis_index("tensor")
    width = w_out.shape[1] // size
    rows = gated.shape[0]
    half = rows // 2

    def term(offset):
        cols = lax.dynamic_slice_in_dim(w_out, ((index + offset) % size) * width, width, 1)
        return jnp.dot(gated, cols, preferred_element_type=jnp.float32).astype(jnp.bfloat16)

    far = term(2)
    far_from_left = ring(far[:half], 1).astype(jnp.float32)
    far_from_right = ring(far[half:], -1).astype(jnp.float32)
    near_right, near_left = term(1), term(-1)
    to_right = jnp.concatenate(
        [(near_right[:half].astype(jnp.float32) + far_from_left).astype(jnp.bfloat16), near_right[half:]]
    )
    to_left = jnp.concatenate(
        [near_left[:half], (near_left[half:].astype(jnp.float32) + far_from_right).astype(jnp.bfloat16)]
    )
    from_left = ring(to_right, 1)
    from_right = ring(to_left, -1)
    total = term(0).astype(jnp.float32) + from_left.astype(jnp.float32)
    total = total + from_right.astype(jnp.float32)
    return total


def body(
    hidden_in,
    segment,
    w_query,
    w_key,
    w_value,
    w_outgate,
    w_gate_down,
    w_gate_up,
    gate_bias,
    norm_gain,
    w_out,
):
    tok_rows = hidden_in.shape[0]
    key_width = w_query.shape[1]
    value_width = w_value.shape[1]
    weights = (w_query, w_key, w_value, w_outgate, w_gate_down)
    query_sum, key_sum, value_sum, outgate, low = projected(*gathered(hidden_in), weights)
    query = query_sum.astype(jnp.bfloat16)
    key = key_sum.astype(jnp.bfloat16)
    value = value_sum.astype(jnp.bfloat16)
    pre_gate = jnp.dot(low, w_gate_up.astype(jnp.float32), precision=HIGHEST) + gate_bias
    logdecay = jax.nn.log_sigmoid(pre_gate) / 16.0

    blocks = tok_rows // GROUP
    starts = jnp.concatenate(
        [jnp.zeros((1,), jnp.int32), (segment[1:] != segment[:-1]).astype(jnp.int32)]
    )
    live_device = (jnp.cumsum(starts) == 0).astype(jnp.float32)
    seg_blocks = segment.reshape(blocks, GROUP)
    live_blocks = (jnp.cumsum(starts.reshape(blocks, GROUP), axis=1) == 0).astype(jnp.float32)
    cumul = jnp.cumsum(logdecay.reshape(blocks, GROUP, key_width), axis=1)
    block_totals = cumul[:, -1, :]
    before = jnp.cumsum(block_totals, axis=0) - block_totals
    device_cumul = (cumul + before[:, None, :]).reshape(tok_rows, key_width)

    q_float = query.astype(jnp.float32).reshape(blocks, GROUP, key_width)
    k_float = key.astype(jnp.float32).reshape(blocks, GROUP, key_width)
    v_float = value.astype(jnp.float32).reshape(blocks, GROUP, value_width)

    positions = jnp.arange(GROUP)
    causal = positions[None, :] <= positions[:, None]
    centre = cumul[:, GROUP // 2, :]
    q_scaled = q_float * jnp.exp(cumul - centre[:, None, :])
    k_scaled = k_float * jnp.exp(centre[:, None, :] - cumul)
    raw_scores = jnp.einsum("ncd,nsd->ncs", q_scaled, k_scaled, precision=HIGH)
    allowed = causal[None] & (seg_blocks[:, :, None] == seg_blocks[:, None, :])
    scores = jnp.where(allowed, raw_scores, 0.0)
    intra = jnp.einsum("ncs,nsv->ncv", scores, v_float, precision=HIGH)

    same_last = (seg_blocks == seg_blocks[:, -1:]).astype(jnp.float32)
    k_decayed = k_float * jnp.exp(block_totals[:, None, :] - cumul) * same_last[:, :, None]
    chunk_states = jnp.einsum("ncd,ncv->ndv", k_decayed, v_float, precision=HIGH)
    chunk_decay = jnp.exp(block_totals) * live_blocks[:, -1:]

    q_decayed = q_float * jnp.exp(cumul)
    entering = jnp.zeros((key_width, value_width), jnp.float32)
    inters = []
    for n in range(blocks):
        inters.append(jnp.dot(q_decayed[n], entering, precision=HIGH))
        entering = chunk_decay[n][:, None] * entering + chunk_states[n]
    final_state = entering
    inter = jnp.stack(inters) * live_blocks[:, :, None]
    local_out = (intra + inter).reshape(tok_rows, value_width)

    devices = lax.axis_size("req")
    window = min(devices - 1, -(-SEG_MOST // tok_rows))
    first_id = (segment[0] + 1).astype(jnp.float32)
    last_id = (segment[-1] + 1).astype(jnp.float32)
    decay_device = jnp.exp(device_cumul[-1]) * live_device[-1]
    tail = jnp.zeros((2, value_width), jnp.float32)
    tail = tail.at[0, :key_width].set(decay_device).at[1, 0].set(first_id).at[1, 1].set(last_id)
    message = jnp.concatenate([final_state, tail]).astype(jnp.bfloat16)
    got = [shifted(message, "req", j, devices).astype(jnp.float32) for j in range(1, window + 1)]
    state_in = got[-1][:key_width]
    last_far = got[-1][key_width + 1, 1]
    for j in range(window - 1, 0, -1):
        msg = got[j - 1]
        link = (msg[key_width + 1, 0] == last_far).astype(jnp.float32)
        state_in = msg[:key_width] + (link * msg[key_width, :key_width])[:, None] * state_in
        last_far = msg[key_width + 1, 1]
    linked = (first_id == last_far).astype(jnp.float32)
    carried = jnp.dot(
        query.astype(jnp.float32) * jnp.exp(device_cumul), state_in, precision=HIGH
    )
    attn = (local_out + carried * (live_device * linked)[:, None]) * key_width ** (-0.5)
    normed = attn * lax.rsqrt(jnp.mean(attn * attn, axis=-1, keepdims=True) + 1e-05) * norm_gain
    gated = (normed * jax.nn.silu(outgate)).astype(jnp.bfloat16)
    return scattered_sum(gated, w_out).astype(jnp.bfloat16)


def solution(mesh):
    in_specs = (
        P("req", "tensor"),
        P("req"),
        P(None, "tensor"),
        P(None, "tensor"),
        P(None, "tensor"),
        P(None, "tensor"),
        P(),
        P(None, "tensor"),
        P("tensor"),
        P(),
        P("tensor", None),
    )
    out_specs = P("req", "tensor")
    return jax.shard_map(body, mesh=mesh, in_specs=in_specs, out_specs=out_specs, check_vma=False)
```

```python
import jax
import jax.numpy as jnp
from jax import lax
from jax.sharding import PartitionSpec as P

GROUP = 64
SEG_MOST = 4096
HIGHEST = lax.Precision.HIGHEST
HIGH = lax.Precision.HIGH


def shifted(x, axis, shift, devices):
    pairs = [(i, i + shift) for i in range(devices - shift)]
    return lax.ppermute(x, axis, pairs)


def ring(x, step):
    size = lax.axis_size("tensor")
    return lax.ppermute(x, "tensor", [(i, (i + step) % size) for i in range(size)])


def gathered(local):
    half = local.shape[0] // 2
    left_a = ring(local[:half], 1)
    right_a = ring(local[half:], -1)
    left_a, right_a, rest = lax.optimization_barrier((left_a, right_a, local))
    left_b = ring(rest[half:], 1)
    right_b = ring(rest[:half], -1)
    far = jnp.concatenate([ring(left_a, 1), ring(right_a, -1)])
    from_left = jnp.concatenate([left_a, left_b])
    from_right = jnp.concatenate([right_b, right_a])
    return jnp.concatenate([local, from_right, from_left], axis=1), far


def projected(near, far, weights):
    size = lax.axis_size("tensor")
    index = lax.axis_index("tensor")
    width = far.shape[1]
    parts = []
    for weight in weights:

        def rows(offset):
            return lax.dynamic_slice_in_dim(weight, ((index + offset) % size) * width, width, 0)

        near_rows = jnp.concatenate([rows(0), rows(1), rows(size - 1)])
        out = jnp.dot(near, near_rows, preferred_element_type=jnp.float32)
        parts.append(out + jnp.dot(far, rows(2), preferred_element_type=jnp.float32))
    return parts


def scattered_sum(gated, w_out):
    size = lax.axis_size("tensor")
    index = lax.axis_index("tensor")
    width = w_out.shape[1] // size
    rows = gated.shape[0]
    half = rows // 2

    def term(offset):
        cols = lax.dynamic_slice_in_dim(w_out, ((index + offset) % size) * width, width, 1)
        return jnp.dot(gated, cols, preferred_element_type=jnp.float32).astype(jnp.bfloat16)

    far = term(2)
    far_from_left = ring(far[:half], 1).astype(jnp.float32)
    far_from_right = ring(far[half:], -1).astype(jnp.float32)
    near_right, near_left = term(1), term(-1)
    to_right = jnp.concatenate(
        [(near_right[:half].astype(jnp.float32) + far_from_left).astype(jnp.bfloat16), near_right[half:]]
    )
    to_left = jnp.concatenate(
        [near_left[:half], (near_left[half:].astype(jnp.float32) + far_from_right).astype(jnp.bfloat16)]
    )
    from_left = ring(to_right, 1)
    from_right = ring(to_left, -1)
    total = term(0).astype(jnp.float32) + from_left.astype(jnp.float32)
    total = total + from_right.astype(jnp.float32)
    return total


def body(
    hidden_in,
    segment,
    w_query,
    w_key,
    w_value,
    w_outgate,
    w_gate_down,
    w_gate_up,
    gate_bias,
    norm_gain,
    w_out,
):
    tok_rows = hidden_in.shape[0]
    key_width = w_query.shape[1]
    value_width = w_value.shape[1]
    weights = (w_query, w_key, w_value, w_outgate, w_gate_down)
    query_sum, key_sum, value_sum, outgate, low = projected(*gathered(hidden_in), weights)
    query = query_sum.astype(jnp.bfloat16)
    key = key_sum.astype(jnp.bfloat16)
    value = value_sum.astype(jnp.bfloat16)
    pre_gate = jnp.dot(low, w_gate_up.astype(jnp.float32), precision=HIGHEST) + gate_bias
    logdecay = jax.nn.log_sigmoid(pre_gate) / 16.0

    blocks = tok_rows // GROUP
    starts = jnp.concatenate(
        [jnp.zeros((1,), jnp.int32), (segment[1:] != segment[:-1]).astype(jnp.int32)]
    )
    live_device = (jnp.cumsum(starts) == 0).astype(jnp.float32)
    seg_blocks = segment.reshape(blocks, GROUP)
    live_blocks = (jnp.cumsum(starts.reshape(blocks, GROUP), axis=1) == 0).astype(jnp.float32)
    cumul = jnp.cumsum(logdecay.reshape(blocks, GROUP, key_width), axis=1)
    block_totals = cumul[:, -1, :]
    before = jnp.cumsum(block_totals, axis=0) - block_totals
    device_cumul = (cumul + before[:, None, :]).reshape(tok_rows, key_width)

    q_float = query.astype(jnp.float32).reshape(blocks, GROUP, key_width)
    k_float = key.astype(jnp.float32).reshape(blocks, GROUP, key_width)
    v_float = value.astype(jnp.float32).reshape(blocks, GROUP, value_width)

    positions = jnp.arange(GROUP)
    causal = positions[None, :] <= positions[:, None]
    centre = cumul[:, GROUP // 2, :]
    q_scaled = q_float * jnp.exp(cumul - centre[:, None, :])
    k_scaled = k_float * jnp.exp(centre[:, None, :] - cumul)
    raw_scores = jnp.einsum("ncd,nsd->ncs", q_scaled, k_scaled, precision=HIGH)
    allowed = causal[None] & (seg_blocks[:, :, None] == seg_blocks[:, None, :])
    scores = jnp.where(allowed, raw_scores, 0.0)
    intra = jnp.einsum("ncs,nsv->ncv", scores, v_float, precision=HIGH)

    same_last = (seg_blocks == seg_blocks[:, -1:]).astype(jnp.float32)
    k_decayed = k_float * jnp.exp(block_totals[:, None, :] - cumul) * same_last[:, :, None]
    chunk_states = jnp.einsum("ncd,ncv->ndv", k_decayed, v_float, precision=HIGH)
    chunk_decay = jnp.exp(block_totals) * live_blocks[:, -1:]

    q_decayed = q_float * jnp.exp(cumul)
    entering = jnp.zeros((key_width, value_width), jnp.float32)
    inters = []
    for n in range(blocks):
        inters.append(jnp.dot(q_decayed[n], entering, precision=HIGH))
        entering = chunk_decay[n][:, None] * entering + chunk_states[n]
    final_state = entering
    inter = jnp.stack(inters) * live_blocks[:, :, None]
    local_out = (intra + inter).reshape(tok_rows, value_width)

    devices = lax.axis_size("req")
    window = min(devices - 1, -(-SEG_MOST // tok_rows))
    first_id = (segment[0] + 1).astype(jnp.float32)
    last_id = (segment[-1] + 1).astype(jnp.float32)
    decay_device = jnp.exp(device_cumul[-1]) * live_device[-1]
    tail = jnp.zeros((2, value_width), jnp.float32)
    tail = tail.at[0, :key_width].set(decay_device).at[1, 0].set(first_id).at[1, 1].set(last_id)
    message = jnp.concatenate([final_state, tail]).astype(jnp.bfloat16)
    def unpack(msg):
        return msg[:key_width], msg[key_width, :key_width], msg[key_width + 1, 0], msg[key_width + 1, 1]

    def joined(earlier, later):
        state_a, decay_a, first_a, last_a = earlier
        state_b, decay_b, first_b, last_b = later
        link = (first_b == last_a).astype(jnp.float32)
        return (state_b + (link * decay_b)[:, None] * state_a, decay_a * decay_b * link, first_a, last_b)

    assert window == 4
    pair = joined(
        unpack(shifted(message, "req", 2, devices).astype(jnp.float32)),
        unpack(shifted(message, "req", 1, devices).astype(jnp.float32)),
    )
    pair_state, pair_decay, pair_first, pair_last = pair
    pair_tail = jnp.zeros((2, value_width), jnp.float32)
    pair_tail = pair_tail.at[0, :key_width].set(pair_decay).at[1, 0].set(pair_first)
    pair_tail = pair_tail.at[1, 1].set(pair_last)
    pair_message = jnp.concatenate([pair_state, pair_tail]).astype(jnp.bfloat16)
    earlier_pair = unpack(shifted(pair_message, "req", 2, devices).astype(jnp.float32))
    state_in, _, _, last_far = joined(earlier_pair, pair)
    linked = (first_id == last_far).astype(jnp.float32)
    carried = jnp.dot(
        query.astype(jnp.float32) * jnp.exp(device_cumul), state_in, precision=HIGH
    )
    attn = (local_out + carried * (live_device * linked)[:, None]) * key_width ** (-0.5)
    normed = attn * lax.rsqrt(jnp.mean(attn * attn, axis=-1, keepdims=True) + 1e-05) * norm_gain
    gated = (normed * jax.nn.silu(outgate)).astype(jnp.bfloat16)
    return scattered_sum(gated, w_out).astype(jnp.bfloat16)


def solution(mesh):
    in_specs = (
        P("req", "tensor"),
        P("req"),
        P(None, "tensor"),
        P(None, "tensor"),
        P(None, "tensor"),
        P(None, "tensor"),
        P(),
        P(None, "tensor"),
        P("tensor"),
        P(),
        P("tensor", None),
    )
    out_specs = P("req", "tensor")
    return jax.shard_map(body, mesh=mesh, in_specs=in_specs, out_specs=out_specs, check_vma=False)
```

```python
import jax
import jax.numpy as jnp
from jax import lax
from jax.sharding import PartitionSpec as P

GROUP = 64
SEG_MOST = 4096
HIGHEST = lax.Precision.HIGHEST
HIGH = lax.Precision.HIGH


def shifted(x, axis, shift, devices):
    pairs = [(i, i + shift) for i in range(devices - shift)]
    return lax.ppermute(x, axis, pairs)


def split_dot(spec, a, b):
    high = a.astype(jnp.bfloat16)
    low = (a - high.astype(jnp.float32)).astype(jnp.bfloat16)
    first = jnp.einsum(spec, high, b, preferred_element_type=jnp.float32)
    return first + jnp.einsum(spec, low, b, preferred_element_type=jnp.float32)


def ring(x, step):
    size = lax.axis_size("tensor")
    return lax.ppermute(x, "tensor", [(i, (i + step) % size) for i in range(size)])


def gathered(local):
    half = local.shape[0] // 2
    left_a = ring(local[:half], 1)
    right_a = ring(local[half:], -1)
    left_a, right_a, rest = lax.optimization_barrier((left_a, right_a, local))
    left_b = ring(rest[half:], 1)
    right_b = ring(rest[:half], -1)
    far = jnp.concatenate([ring(left_a, 1), ring(right_a, -1)])
    from_left = jnp.concatenate([left_a, left_b])
    from_right = jnp.concatenate([right_b, right_a])
    return jnp.concatenate([local, from_right, from_left], axis=1), far


def projected(near, far, weights):
    size = lax.axis_size("tensor")
    index = lax.axis_index("tensor")
    width = far.shape[1]
    parts = []
    for weight in weights:

        def rows(offset):
            return lax.dynamic_slice_in_dim(weight, ((index + offset) % size) * width, width, 0)

        near_rows = jnp.concatenate([rows(0), rows(1), rows(size - 1)])
        out = jnp.dot(near, near_rows, preferred_element_type=jnp.float32)
        parts.append(out + jnp.dot(far, rows(2), preferred_element_type=jnp.float32))
    return parts


def scattered_sum(gated, w_out):
    size = lax.axis_size("tensor")
    index = lax.axis_index("tensor")
    width = w_out.shape[1] // size
    rows = gated.shape[0]
    half = rows // 2

    def term(offset):
        cols = lax.dynamic_slice_in_dim(w_out, ((index + offset) % size) * width, width, 1)
        return jnp.dot(gated, cols, preferred_element_type=jnp.float32).astype(jnp.bfloat16)

    far = term(2)
    far_from_left = ring(far[:half], 1).astype(jnp.float32)
    far_from_right = ring(far[half:], -1).astype(jnp.float32)
    near_right, near_left = term(1), term(-1)
    to_right = jnp.concatenate(
        [(near_right[:half].astype(jnp.float32) + far_from_left).astype(jnp.bfloat16), near_right[half:]]
    )
    to_left = jnp.concatenate(
        [near_left[:half], (near_left[half:].astype(jnp.float32) + far_from_right).astype(jnp.bfloat16)]
    )
    from_left = ring(to_right, 1)
    from_right = ring(to_left, -1)
    total = term(0).astype(jnp.float32) + from_left.astype(jnp.float32)
    total = total + from_right.astype(jnp.float32)
    return total


def body(
    hidden_in,
    segment,
    w_query,
    w_key,
    w_value,
    w_outgate,
    w_gate_down,
    w_gate_up,
    gate_bias,
    norm_gain,
    w_out,
):
    tok_rows = hidden_in.shape[0]
    key_width = w_query.shape[1]
    value_width = w_value.shape[1]
    weights = (w_query, w_key, w_value, w_outgate, w_gate_down)
    query_sum, key_sum, value_sum, outgate, low = projected(*gathered(hidden_in), weights)
    query = query_sum.astype(jnp.bfloat16)
    key = key_sum.astype(jnp.bfloat16)
    value = value_sum.astype(jnp.bfloat16)
    pre_gate = jnp.dot(low, w_gate_up.astype(jnp.float32), precision=HIGHEST) + gate_bias
    logdecay = jax.nn.log_sigmoid(pre_gate) / 16.0

    blocks = tok_rows // GROUP
    starts = jnp.concatenate(
        [jnp.zeros((1,), jnp.int32), (segment[1:] != segment[:-1]).astype(jnp.int32)]
    )
    live_device = (jnp.cumsum(starts) == 0).astype(jnp.float32)
    seg_blocks = segment.reshape(blocks, GROUP)
    live_blocks = (jnp.cumsum(starts.reshape(blocks, GROUP), axis=1) == 0).astype(jnp.float32)
    cumul = jnp.cumsum(logdecay.reshape(blocks, GROUP, key_width), axis=1)
    block_totals = cumul[:, -1, :]
    before = jnp.cumsum(block_totals, axis=0) - block_totals
    device_cumul = (cumul + before[:, None, :]).reshape(tok_rows, key_width)

    q_float = query.astype(jnp.float32).reshape(blocks, GROUP, key_width)
    k_float = key.astype(jnp.float32).reshape(blocks, GROUP, key_width)
    v_blocks = value.reshape(blocks, GROUP, value_width)

    positions = jnp.arange(GROUP)
    causal = positions[None, :] <= positions[:, None]
    centre = cumul[:, GROUP // 2, :]
    q_scaled = q_float * jnp.exp(cumul - centre[:, None, :])
    k_scaled = k_float * jnp.exp(centre[:, None, :] - cumul)
    raw_scores = jnp.einsum("ncd,nsd->ncs", q_scaled, k_scaled, precision=HIGH)
    allowed = causal[None] & (seg_blocks[:, :, None] == seg_blocks[:, None, :])
    scores = jnp.where(allowed, raw_scores, 0.0)
    intra = split_dot("ncs,nsv->ncv", scores, v_blocks)

    same_last = (seg_blocks == seg_blocks[:, -1:]).astype(jnp.float32)
    k_decayed = k_float * jnp.exp(block_totals[:, None, :] - cumul) * same_last[:, :, None]
    chunk_states = split_dot("ncd,ncv->ndv", k_decayed, v_blocks)
    chunk_decay = jnp.exp(block_totals) * live_blocks[:, -1:]

    q_decayed = q_float * jnp.exp(cumul)
    entering = jnp.zeros((key_width, value_width), jnp.float32)
    inters = []
    for n in range(blocks):
        inters.append(jnp.dot(q_decayed[n], entering, precision=HIGH))
        entering = chunk_decay[n][:, None] * entering + chunk_states[n]
    final_state = entering
    inter = jnp.stack(inters) * live_blocks[:, :, None]
    local_out = (intra + inter).reshape(tok_rows, value_width)

    devices = lax.axis_size("req")
    window = min(devices - 1, -(-SEG_MOST // tok_rows))
    first_id = (segment[0] + 1).astype(jnp.float32)
    last_id = (segment[-1] + 1).astype(jnp.float32)
    decay_device = jnp.exp(device_cumul[-1]) * live_device[-1]
    tail = jnp.zeros((2, value_width), jnp.float32)
    tail = tail.at[0, :key_width].set(decay_device).at[1, 0].set(first_id).at[1, 1].set(last_id)
    message = jnp.concatenate([final_state, tail]).astype(jnp.bfloat16)
    def unpack(msg):
        return msg[:key_width], msg[key_width, :key_width], msg[key_width + 1, 0], msg[key_width + 1, 1]

    def joined(earlier, later):
        state_a, decay_a, first_a, last_a = earlier
        state_b, decay_b, first_b, last_b = later
        link = (first_b == last_a).astype(jnp.float32)
        return (state_b + (link * decay_b)[:, None] * state_a, decay_a * decay_b * link, first_a, last_b)

    assert window == 4
    pair = joined(
        unpack(shifted(message, "req", 2, devices).astype(jnp.float32)),
        unpack(shifted(message, "req", 1, devices).astype(jnp.float32)),
    )
    pair_state, pair_decay, pair_first, pair_last = pair
    pair_tail = jnp.zeros((2, value_width), jnp.float32)
    pair_tail = pair_tail.at[0, :key_width].set(pair_decay).at[1, 0].set(pair_first)
    pair_tail = pair_tail.at[1, 1].set(pair_last)
    pair_message = jnp.concatenate([pair_state, pair_tail]).astype(jnp.bfloat16)
    earlier_pair = unpack(shifted(pair_message, "req", 2, devices).astype(jnp.float32))
    state_in, _, _, last_far = joined(earlier_pair, pair)
    linked = (first_id == last_far).astype(jnp.float32)
    carried = jnp.dot(
        query.astype(jnp.float32) * jnp.exp(device_cumul), state_in, precision=HIGH
    )
    attn = (local_out + carried * (live_device * linked)[:, None]) * key_width ** (-0.5)
    normed = attn * lax.rsqrt(jnp.mean(attn * attn, axis=-1, keepdims=True) + 1e-05) * norm_gain
    gated = (normed * jax.nn.silu(outgate)).astype(jnp.bfloat16)
    return scattered_sum(gated, w_out).astype(jnp.bfloat16)


def solution(mesh):
    in_specs = (
        P("req", "tensor"),
        P("req"),
        P(None, "tensor"),
        P(None, "tensor"),
        P(None, "tensor"),
        P(None, "tensor"),
        P(),
        P(None, "tensor"),
        P("tensor"),
        P(),
        P("tensor", None),
    )
    out_specs = P("req", "tensor")
    return jax.shard_map(body, mesh=mesh, in_specs=in_specs, out_specs=out_specs, check_vma=False)
```

```python
import jax
import jax.numpy as jnp
from jax import lax
from jax.sharding import PartitionSpec as P

GROUP = 64
SEG_MOST = 4096
HIGHEST = lax.Precision.HIGHEST
HIGH = lax.Precision.HIGH


def shifted(x, axis, shift, devices):
    pairs = [(i, i + shift) for i in range(devices - shift)]
    return lax.ppermute(x, axis, pairs)


def ring(x, step):
    size = lax.axis_size("tensor")
    return lax.ppermute(x, "tensor", [(i, (i + step) % size) for i in range(size)])


def gathered(local):
    half = local.shape[0] // 2
    left_a = ring(local[:half], 1)
    right_a = ring(local[half:], -1)
    left_a, right_a, rest = lax.optimization_barrier((left_a, right_a, local))
    left_b = ring(rest[half:], 1)
    right_b = ring(rest[:half], -1)
    far = jnp.concatenate([ring(left_a, 1), ring(right_a, -1)])
    from_left = jnp.concatenate([left_a, left_b])
    from_right = jnp.concatenate([right_b, right_a])
    return jnp.concatenate([local, from_right, from_left], axis=1), far


def projected(near, far, weights):
    size = lax.axis_size("tensor")
    index = lax.axis_index("tensor")
    width = far.shape[1]
    parts = []
    for weight in weights:

        def rows(offset):
            return lax.dynamic_slice_in_dim(weight, ((index + offset) % size) * width, width, 0)

        near_rows = jnp.concatenate([rows(0), rows(1), rows(size - 1)])
        out = jnp.dot(near, near_rows, preferred_element_type=jnp.float32)
        parts.append(out + jnp.dot(far, rows(2), preferred_element_type=jnp.float32))
    return parts


def scattered_sum(gated, w_out):
    size = lax.axis_size("tensor")
    index = lax.axis_index("tensor")
    width = w_out.shape[1] // size
    rows = gated.shape[0]
    half = rows // 2

    def term(offset):
        cols = lax.dynamic_slice_in_dim(w_out, ((index + offset) % size) * width, width, 1)
        return jnp.dot(gated, cols, preferred_element_type=jnp.float32).astype(jnp.bfloat16)

    far = term(2)
    far_from_left = ring(far[:half], 1).astype(jnp.float32)
    far_from_right = ring(far[half:], -1).astype(jnp.float32)
    near_right, near_left = term(1), term(-1)
    to_right = jnp.concatenate(
        [(near_right[:half].astype(jnp.float32) + far_from_left).astype(jnp.bfloat16), near_right[half:]]
    )
    to_left = jnp.concatenate(
        [near_left[:half], (near_left[half:].astype(jnp.float32) + far_from_right).astype(jnp.bfloat16)]
    )
    from_left = ring(to_right, 1)
    from_right = ring(to_left, -1)
    total = term(0).astype(jnp.float32) + from_left.astype(jnp.float32)
    total = total + from_right.astype(jnp.float32)
    return total


def body(
    hidden_in,
    segment,
    w_query,
    w_key,
    w_value,
    w_outgate,
    w_gate_down,
    w_gate_up,
    gate_bias,
    norm_gain,
    w_out,
):
    tok_rows = hidden_in.shape[0]
    key_width = w_query.shape[1]
    value_width = w_value.shape[1]
    weights = (w_query, w_key, w_value, w_outgate, w_gate_down)
    query_sum, key_sum, value_sum, outgate, low = projected(*gathered(hidden_in), weights)
    query = query_sum.astype(jnp.bfloat16)
    key = key_sum.astype(jnp.bfloat16)
    value = value_sum.astype(jnp.bfloat16)
    pre_gate = jnp.dot(low, w_gate_up.astype(jnp.float32), precision=HIGHEST) + gate_bias
    logdecay = jax.nn.log_sigmoid(pre_gate) / 16.0

    blocks = tok_rows // GROUP
    starts = jnp.concatenate(
        [jnp.zeros((1,), jnp.int32), (segment[1:] != segment[:-1]).astype(jnp.int32)]
    )
    live_device = (jnp.cumsum(starts) == 0).astype(jnp.float32)
    seg_blocks = segment.reshape(blocks, GROUP)
    live_blocks = (jnp.cumsum(starts.reshape(blocks, GROUP), axis=1) == 0).astype(jnp.float32)
    cumul = jnp.cumsum(logdecay.reshape(blocks, GROUP, key_width), axis=1)
    block_totals = cumul[:, -1, :]
    before = jnp.cumsum(block_totals, axis=0) - block_totals
    device_cumul = (cumul + before[:, None, :]).reshape(tok_rows, key_width)

    q_float = query.astype(jnp.float32).reshape(blocks, GROUP, key_width)
    k_float = key.astype(jnp.float32).reshape(blocks, GROUP, key_width)
    v_float = value.astype(jnp.float32).reshape(blocks, GROUP, value_width)

    positions = jnp.arange(GROUP)
    causal = positions[None, :] <= positions[:, None]
    centre = cumul[:, GROUP // 2, :]
    q_scaled = q_float * jnp.exp(cumul - centre[:, None, :])
    k_scaled = k_float * jnp.exp(centre[:, None, :] - cumul)
    raw_scores = jnp.einsum("ncd,nsd->ncs", q_scaled, k_scaled, precision=HIGH)
    allowed = causal[None] & (seg_blocks[:, :, None] == seg_blocks[:, None, :])
    scores = jnp.where(allowed, raw_scores, 0.0)
    intra = jnp.einsum("ncs,nsv->ncv", scores, v_float, precision=HIGH)

    same_last = (seg_blocks == seg_blocks[:, -1:]).astype(jnp.float32)
    k_decayed = k_float * jnp.exp(block_totals[:, None, :] - cumul) * same_last[:, :, None]
    chunk_states = jnp.einsum("ncd,ncv->ndv", k_decayed, v_float, precision=HIGH)
    chunk_decay = jnp.exp(block_totals) * live_blocks[:, -1:]

    q_decayed = q_float * jnp.exp(cumul)
    zero_row = jnp.zeros((1, key_width), jnp.float32)
    totals_before = jnp.concatenate([zero_row, jnp.cumsum(block_totals, axis=0)])
    dead = 1.0 - live_blocks[:, -1]
    dead_before = jnp.concatenate([jnp.zeros((1,), jnp.float32), jnp.cumsum(dead)])
    ends = jnp.arange(blocks + 1)[:, None]
    sources = jnp.arange(blocks)[None, :]
    valid = (sources < ends) & (dead_before[:, None] == dead_before[None, 1:])
    exponent = totals_before[:, None, :] - totals_before[None, 1:, :]
    exponent = jnp.where(valid[:, :, None], exponent, 0.0)
    weight = jnp.where(valid[:, :, None], jnp.exp(exponent), 0.0)
    entering = jnp.einsum("nmk,mkv->nkv", weight, chunk_states, precision=HIGH)
    final_state = entering[blocks]
    inter = (
        jnp.einsum("ncd,ndv->ncv", q_decayed, entering[:blocks], precision=HIGH)
        * live_blocks[:, :, None]
    )
    local_out = (intra + inter).reshape(tok_rows, value_width)

    devices = lax.axis_size("req")
    window = min(devices - 1, -(-SEG_MOST // tok_rows))
    first_id = (segment[0] + 1).astype(jnp.float32)
    last_id = (segment[-1] + 1).astype(jnp.float32)
    decay_device = jnp.exp(device_cumul[-1]) * live_device[-1]
    tail = jnp.zeros((2, value_width), jnp.float32)
    tail = tail.at[0, :key_width].set(decay_device).at[1, 0].set(first_id).at[1, 1].set(last_id)
    message = jnp.concatenate([final_state, tail]).astype(jnp.bfloat16)
    def unpack(msg):
        return msg[:key_width], msg[key_width, :key_width], msg[key_width + 1, 0], msg[key_width + 1, 1]

    def joined(earlier, later):
        state_a, decay_a, first_a, last_a = earlier
        state_b, decay_b, first_b, last_b = later
        link = (first_b == last_a).astype(jnp.float32)
        return (state_b + (link * decay_b)[:, None] * state_a, decay_a * decay_b * link, first_a, last_b)

    assert window == 4
    pair = joined(
        unpack(shifted(message, "req", 2, devices).astype(jnp.float32)),
        unpack(shifted(message, "req", 1, devices).astype(jnp.float32)),
    )
    pair_state, pair_decay, pair_first, pair_last = pair
    pair_tail = jnp.zeros((2, value_width), jnp.float32)
    pair_tail = pair_tail.at[0, :key_width].set(pair_decay).at[1, 0].set(pair_first)
    pair_tail = pair_tail.at[1, 1].set(pair_last)
    pair_message = jnp.concatenate([pair_state, pair_tail]).astype(jnp.bfloat16)
    earlier_pair = unpack(shifted(pair_message, "req", 2, devices).astype(jnp.float32))
    state_in, _, _, last_far = joined(earlier_pair, pair)
    linked = (first_id == last_far).astype(jnp.float32)
    carried = jnp.dot(
        query.astype(jnp.float32) * jnp.exp(device_cumul), state_in, precision=HIGH
    )
    attn = (local_out + carried * (live_device * linked)[:, None]) * key_width ** (-0.5)
    normed = attn * lax.rsqrt(jnp.mean(attn * attn, axis=-1, keepdims=True) + 1e-05) * norm_gain
    gated = (normed * jax.nn.silu(outgate)).astype(jnp.bfloat16)
    return scattered_sum(gated, w_out).astype(jnp.bfloat16)


def solution(mesh):
    in_specs = (
        P("req", "tensor"),
        P("req"),
        P(None, "tensor"),
        P(None, "tensor"),
        P(None, "tensor"),
        P(None, "tensor"),
        P(),
        P(None, "tensor"),
        P("tensor"),
        P(),
        P("tensor", None),
    )
    out_specs = P("req", "tensor")
    return jax.shard_map(body, mesh=mesh, in_specs=in_specs, out_specs=out_specs, check_vma=False)
```

```python
import jax
import jax.numpy as jnp
from jax import lax
from jax.sharding import PartitionSpec as P

GROUP = 64
SEG_MOST = 4096
HIGHEST = lax.Precision.HIGHEST
HIGH = lax.Precision.HIGH


def shifted(x, axis, shift, devices):
    pairs = [(i, i + shift) for i in range(devices - shift)]
    return lax.ppermute(x, axis, pairs)


def ring(x, step):
    size = lax.axis_size("tensor")
    return lax.ppermute(x, "tensor", [(i, (i + step) % size) for i in range(size)])


def gathered(local):
    half = local.shape[0] // 2
    left_a = ring(local[:half], 1)
    right_a = ring(local[half:], -1)
    left_a, right_a, rest = lax.optimization_barrier((left_a, right_a, local))
    left_b = ring(rest[half:], 1)
    right_b = ring(rest[:half], -1)
    far = jnp.concatenate([ring(left_a, 1), ring(right_a, -1)])
    from_left = jnp.concatenate([left_a, left_b])
    from_right = jnp.concatenate([right_b, right_a])
    return jnp.concatenate([local, from_right, from_left], axis=1), far


def projected(near, far, weights):
    size = lax.axis_size("tensor")
    index = lax.axis_index("tensor")
    width = far.shape[1]
    parts = []
    for weight in weights:

        def rows(offset):
            return lax.dynamic_slice_in_dim(weight, ((index + offset) % size) * width, width, 0)

        near_rows = jnp.concatenate([rows(0), rows(1), rows(size - 1)])
        out = jnp.dot(near, near_rows, preferred_element_type=jnp.float32)
        parts.append(out + jnp.dot(far, rows(2), preferred_element_type=jnp.float32))
    return parts


def scattered_sum(gated, w_out):
    size = lax.axis_size("tensor")
    index = lax.axis_index("tensor")
    width = w_out.shape[1] // size
    rows = gated.shape[0]
    half = rows // 2

    def term(offset):
        cols = lax.dynamic_slice_in_dim(w_out, ((index + offset) % size) * width, width, 1)
        return jnp.dot(gated, cols, preferred_element_type=jnp.float32).astype(jnp.bfloat16)

    far = term(2)
    far_from_left = ring(far[:half], 1).astype(jnp.float32)
    far_from_right = ring(far[half:], -1).astype(jnp.float32)
    near_right, near_left = term(1), term(-1)
    to_right = jnp.concatenate(
        [(near_right[:half].astype(jnp.float32) + far_from_left).astype(jnp.bfloat16), near_right[half:]]
    )
    to_left = jnp.concatenate(
        [near_left[:half], (near_left[half:].astype(jnp.float32) + far_from_right).astype(jnp.bfloat16)]
    )
    from_left = ring(to_right, 1)
    from_right = ring(to_left, -1)
    total = term(0).astype(jnp.float32) + from_left.astype(jnp.float32)
    total = total + from_right.astype(jnp.float32)
    return total


def body(
    hidden_in,
    segment,
    w_query,
    w_key,
    w_value,
    w_outgate,
    w_gate_down,
    w_gate_up,
    gate_bias,
    norm_gain,
    w_out,
):
    tok_rows = hidden_in.shape[0]
    key_width = w_query.shape[1]
    value_width = w_value.shape[1]
    weights = (w_query, w_key, w_value, w_outgate, w_gate_down)
    query_sum, key_sum, value_sum, outgate, low = projected(*gathered(hidden_in), weights)
    query = query_sum.astype(jnp.bfloat16)
    key = key_sum.astype(jnp.bfloat16)
    value = value_sum.astype(jnp.bfloat16)
    pre_gate = jnp.dot(low, w_gate_up.astype(jnp.float32), precision=HIGHEST) + gate_bias
    logdecay = jax.nn.log_sigmoid(pre_gate) / 16.0

    blocks = tok_rows // GROUP
    starts = jnp.concatenate(
        [jnp.zeros((1,), jnp.int32), (segment[1:] != segment[:-1]).astype(jnp.int32)]
    )
    live_device = (jnp.cumsum(starts) == 0).astype(jnp.float32)
    seg_blocks = segment.reshape(blocks, GROUP)
    live_blocks = (jnp.cumsum(starts.reshape(blocks, GROUP), axis=1) == 0).astype(jnp.float32)
    cumul = jnp.cumsum(logdecay.reshape(blocks, GROUP, key_width), axis=1)
    block_totals = cumul[:, -1, :]
    before = jnp.cumsum(block_totals, axis=0) - block_totals
    device_cumul = (cumul + before[:, None, :]).reshape(tok_rows, key_width)

    q_float = query.astype(jnp.float32).reshape(blocks, GROUP, key_width)
    k_float = key.astype(jnp.float32).reshape(blocks, GROUP, key_width)
    v_float = value.astype(jnp.float32).reshape(blocks, GROUP, value_width)

    positions = jnp.arange(GROUP)
    causal = positions[None, :] <= positions[:, None]
    centre = cumul[:, GROUP // 2, :]
    q_scaled = q_float * jnp.exp(cumul - centre[:, None, :])
    k_scaled = k_float * jnp.exp(centre[:, None, :] - cumul)
    raw_scores = jnp.einsum("ncd,nsd->ncs", q_scaled, k_scaled, precision=HIGH)
    allowed = causal[None] & (seg_blocks[:, :, None] == seg_blocks[:, None, :])
    scores = jnp.where(allowed, raw_scores, 0.0)
    intra = jnp.einsum("ncs,nsv->ncv", scores, v_float, precision=HIGH)

    same_last = (seg_blocks == seg_blocks[:, -1:]).astype(jnp.float32)
    k_decayed = k_float * jnp.exp(block_totals[:, None, :] - cumul) * same_last[:, :, None]
    chunk_states = jnp.einsum("ncd,ncv->ndv", k_decayed, v_float, precision=HIGH)
    chunk_decay = jnp.exp(block_totals) * live_blocks[:, -1:]

    q_decayed = q_float * jnp.exp(cumul)
    entering = jnp.zeros((key_width, value_width), jnp.float32)
    inters = []
    for n in range(blocks):
        inters.append(
            jnp.dot(
                q_decayed[n].astype(jnp.bfloat16),
                entering.astype(jnp.bfloat16),
                preferred_element_type=jnp.float32,
            )
        )
        entering = chunk_decay[n][:, None] * entering + chunk_states[n]
    final_state = entering
    inter = jnp.stack(inters) * live_blocks[:, :, None]
    local_out = (intra + inter).reshape(tok_rows, value_width)

    devices = lax.axis_size("req")
    window = min(devices - 1, -(-SEG_MOST // tok_rows))
    first_id = (segment[0] + 1).astype(jnp.float32)
    last_id = (segment[-1] + 1).astype(jnp.float32)
    decay_device = jnp.exp(device_cumul[-1]) * live_device[-1]
    tail = jnp.zeros((2, value_width), jnp.float32)
    tail = tail.at[0, :key_width].set(decay_device).at[1, 0].set(first_id).at[1, 1].set(last_id)
    message = jnp.concatenate([final_state, tail]).astype(jnp.bfloat16)
    def unpack(msg):
        return msg[:key_width], msg[key_width, :key_width], msg[key_width + 1, 0], msg[key_width + 1, 1]

    def joined(earlier, later):
        state_a, decay_a, first_a, last_a = earlier
        state_b, decay_b, first_b, last_b = later
        link = (first_b == last_a).astype(jnp.float32)
        return (state_b + (link * decay_b)[:, None] * state_a, decay_a * decay_b * link, first_a, last_b)

    assert window == 4
    pair = joined(
        unpack(shifted(message, "req", 2, devices).astype(jnp.float32)),
        unpack(shifted(message, "req", 1, devices).astype(jnp.float32)),
    )
    pair_state, pair_decay, pair_first, pair_last = pair
    pair_tail = jnp.zeros((2, value_width), jnp.float32)
    pair_tail = pair_tail.at[0, :key_width].set(pair_decay).at[1, 0].set(pair_first)
    pair_tail = pair_tail.at[1, 1].set(pair_last)
    pair_message = jnp.concatenate([pair_state, pair_tail]).astype(jnp.bfloat16)
    earlier_pair = unpack(shifted(pair_message, "req", 2, devices).astype(jnp.float32))
    state_in, _, _, last_far = joined(earlier_pair, pair)
    linked = (first_id == last_far).astype(jnp.float32)
    carried = jnp.dot(
        query.astype(jnp.float32) * jnp.exp(device_cumul), state_in, precision=HIGH
    )
    attn = (local_out + carried * (live_device * linked)[:, None]) * key_width ** (-0.5)
    normed = attn * lax.rsqrt(jnp.mean(attn * attn, axis=-1, keepdims=True) + 1e-05) * norm_gain
    gated = (normed * jax.nn.silu(outgate)).astype(jnp.bfloat16)
    return scattered_sum(gated, w_out).astype(jnp.bfloat16)


def solution(mesh):
    in_specs = (
        P("req", "tensor"),
        P("req"),
        P(None, "tensor"),
        P(None, "tensor"),
        P(None, "tensor"),
        P(None, "tensor"),
        P(),
        P(None, "tensor"),
        P("tensor"),
        P(),
        P("tensor", None),
    )
    out_specs = P("req", "tensor")
    return jax.shard_map(body, mesh=mesh, in_specs=in_specs, out_specs=out_specs, check_vma=False)
```

```python
import jax
import jax.numpy as jnp
from jax import lax
from jax.sharding import PartitionSpec as P

GROUP = 64
SEG_MOST = 4096
HIGHEST = lax.Precision.HIGHEST
HIGH = lax.Precision.HIGH


def shifted(x, axis, shift, devices):
    pairs = [(i, i + shift) for i in range(devices - shift)]
    return lax.ppermute(x, axis, pairs)


def ring(x, step):
    size = lax.axis_size("tensor")
    return lax.ppermute(x, "tensor", [(i, (i + step) % size) for i in range(size)])


def gathered(local):
    half = local.shape[0] // 2
    left_a = ring(local[:half], 1)
    right_a = ring(local[half:], -1)
    left_a, right_a, rest = lax.optimization_barrier((left_a, right_a, local))
    left_b = ring(rest[half:], 1)
    right_b = ring(rest[:half], -1)
    far = jnp.concatenate([ring(left_a, 1), ring(right_a, -1)])
    from_left = jnp.concatenate([left_a, left_b])
    from_right = jnp.concatenate([right_b, right_a])
    return jnp.concatenate([local, from_right, from_left], axis=1), far


def projected(near, far, weights):
    size = lax.axis_size("tensor")
    index = lax.axis_index("tensor")
    width = far.shape[1]
    parts = []
    for weight in weights:

        def rows(offset):
            return lax.dynamic_slice_in_dim(weight, ((index + offset) % size) * width, width, 0)

        near_rows = jnp.concatenate([rows(0), rows(1), rows(size - 1)])
        out = jnp.dot(near, near_rows, preferred_element_type=jnp.float32)
        parts.append(out + jnp.dot(far, rows(2), preferred_element_type=jnp.float32))
    return parts


def scattered_sum(gated, w_out):
    size = lax.axis_size("tensor")
    index = lax.axis_index("tensor")
    width = w_out.shape[1] // size
    rows = gated.shape[0]
    half = rows // 2

    def term(offset):
        cols = lax.dynamic_slice_in_dim(w_out, ((index + offset) % size) * width, width, 1)
        return jnp.dot(gated, cols, preferred_element_type=jnp.float32).astype(jnp.bfloat16)

    far = term(2)
    far_from_left = ring(far[:half], 1).astype(jnp.float32)
    far_from_right = ring(far[half:], -1).astype(jnp.float32)
    near_right, near_left = term(1), term(-1)
    to_right = jnp.concatenate(
        [(near_right[:half].astype(jnp.float32) + far_from_left).astype(jnp.bfloat16), near_right[half:]]
    )
    to_left = jnp.concatenate(
        [near_left[:half], (near_left[half:].astype(jnp.float32) + far_from_right).astype(jnp.bfloat16)]
    )
    from_left = ring(to_right, 1)
    from_right = ring(to_left, -1)
    total = term(0).astype(jnp.float32) + from_left.astype(jnp.float32)
    total = total + from_right.astype(jnp.float32)
    return total


def body(
    hidden_in,
    segment,
    w_query,
    w_key,
    w_value,
    w_outgate,
    w_gate_down,
    w_gate_up,
    gate_bias,
    norm_gain,
    w_out,
):
    tok_rows = hidden_in.shape[0]
    key_width = w_query.shape[1]
    value_width = w_value.shape[1]
    weights = (w_query, w_key, w_value, w_outgate, w_gate_down)
    query_sum, key_sum, value_sum, outgate, low = projected(*gathered(hidden_in), weights)
    query = query_sum.astype(jnp.bfloat16)
    key = key_sum.astype(jnp.bfloat16)
    value = value_sum.astype(jnp.bfloat16)
    pre_gate = jnp.dot(low, w_gate_up.astype(jnp.float32), precision=HIGHEST) + gate_bias
    logdecay = jax.nn.log_sigmoid(pre_gate) / 16.0

    blocks = tok_rows // GROUP
    starts = jnp.concatenate(
        [jnp.zeros((1,), jnp.int32), (segment[1:] != segment[:-1]).astype(jnp.int32)]
    )
    live_device = (jnp.cumsum(starts) == 0).astype(jnp.float32)
    seg_blocks = segment.reshape(blocks, GROUP)
    live_blocks = (jnp.cumsum(starts.reshape(blocks, GROUP), axis=1) == 0).astype(jnp.float32)
    cumul = jnp.cumsum(logdecay.reshape(blocks, GROUP, key_width), axis=1)
    block_totals = cumul[:, -1, :]
    before = jnp.cumsum(block_totals, axis=0) - block_totals
    device_cumul = (cumul + before[:, None, :]).reshape(tok_rows, key_width)

    q_float = query.astype(jnp.float32).reshape(blocks, GROUP, key_width)
    k_float = key.astype(jnp.float32).reshape(blocks, GROUP, key_width)
    v_float = value.astype(jnp.float32).reshape(blocks, GROUP, value_width)

    positions = jnp.arange(GROUP)
    causal = positions[None, :] <= positions[:, None]
    centre = cumul[:, GROUP // 2, :]
    q_scaled = q_float * jnp.exp(cumul - centre[:, None, :])
    k_scaled = k_float * jnp.exp(centre[:, None, :] - cumul)
    raw_scores = jnp.einsum(
        "ncd,nsd->ncs",
        q_scaled.astype(jnp.bfloat16),
        k_scaled.astype(jnp.bfloat16),
        preferred_element_type=jnp.float32,
    )
    allowed = causal[None] & (seg_blocks[:, :, None] == seg_blocks[:, None, :])
    scores = jnp.where(allowed, raw_scores, 0.0)
    intra = jnp.einsum("ncs,nsv->ncv", scores, v_float, precision=HIGH)

    same_last = (seg_blocks == seg_blocks[:, -1:]).astype(jnp.float32)
    k_decayed = k_float * jnp.exp(block_totals[:, None, :] - cumul) * same_last[:, :, None]
    chunk_states = jnp.einsum("ncd,ncv->ndv", k_decayed, v_float, precision=HIGH)
    chunk_decay = jnp.exp(block_totals) * live_blocks[:, -1:]

    q_decayed = q_float * jnp.exp(cumul)
    entering = jnp.zeros((key_width, value_width), jnp.float32)
    inters = []
    for n in range(blocks):
        inters.append(
            jnp.dot(
                q_decayed[n].astype(jnp.bfloat16),
                entering.astype(jnp.bfloat16),
                preferred_element_type=jnp.float32,
            )
        )
        entering = chunk_decay[n][:, None] * entering + chunk_states[n]
    final_state = entering
    inter = jnp.stack(inters) * live_blocks[:, :, None]
    local_out = (intra + inter).reshape(tok_rows, value_width)

    devices = lax.axis_size("req")
    window = min(devices - 1, -(-SEG_MOST // tok_rows))
    first_id = (segment[0] + 1).astype(jnp.float32)
    last_id = (segment[-1] + 1).astype(jnp.float32)
    decay_device = jnp.exp(device_cumul[-1]) * live_device[-1]
    tail = jnp.zeros((2, value_width), jnp.float32)
    tail = tail.at[0, :key_width].set(decay_device).at[1, 0].set(first_id).at[1, 1].set(last_id)
    message = jnp.concatenate([final_state, tail]).astype(jnp.bfloat16)
    def unpack(msg):
        return msg[:key_width], msg[key_width, :key_width], msg[key_width + 1, 0], msg[key_width + 1, 1]

    def joined(earlier, later):
        state_a, decay_a, first_a, last_a = earlier
        state_b, decay_b, first_b, last_b = later
        link = (first_b == last_a).astype(jnp.float32)
        return (state_b + (link * decay_b)[:, None] * state_a, decay_a * decay_b * link, first_a, last_b)

    assert window == 4
    pair = joined(
        unpack(shifted(message, "req", 2, devices).astype(jnp.float32)),
        unpack(shifted(message, "req", 1, devices).astype(jnp.float32)),
    )
    pair_state, pair_decay, pair_first, pair_last = pair
    pair_tail = jnp.zeros((2, value_width), jnp.float32)
    pair_tail = pair_tail.at[0, :key_width].set(pair_decay).at[1, 0].set(pair_first)
    pair_tail = pair_tail.at[1, 1].set(pair_last)
    pair_message = jnp.concatenate([pair_state, pair_tail]).astype(jnp.bfloat16)
    earlier_pair = unpack(shifted(pair_message, "req", 2, devices).astype(jnp.float32))
    state_in, _, _, last_far = joined(earlier_pair, pair)
    linked = (first_id == last_far).astype(jnp.float32)
    carried = jnp.dot(
        (query.astype(jnp.float32) * jnp.exp(device_cumul)).astype(jnp.bfloat16),
        state_in.astype(jnp.bfloat16),
        preferred_element_type=jnp.float32,
    )
    attn = (local_out + carried * (live_device * linked)[:, None]) * key_width ** (-0.5)
    normed = attn * lax.rsqrt(jnp.mean(attn * attn, axis=-1, keepdims=True) + 1e-05) * norm_gain
    gated = (normed * jax.nn.silu(outgate)).astype(jnp.bfloat16)
    return scattered_sum(gated, w_out).astype(jnp.bfloat16)


def solution(mesh):
    in_specs = (
        P("req", "tensor"),
        P("req"),
        P(None, "tensor"),
        P(None, "tensor"),
        P(None, "tensor"),
        P(None, "tensor"),
        P(),
        P(None, "tensor"),
        P("tensor"),
        P(),
        P("tensor", None),
    )
    out_specs = P("req", "tensor")
    return jax.shard_map(body, mesh=mesh, in_specs=in_specs, out_specs=out_specs, check_vma=False)
```

```python
import jax
import jax.numpy as jnp
from jax import lax
from jax.sharding import PartitionSpec as P

GROUP = 64
SEG_MOST = 4096
HIGHEST = lax.Precision.HIGHEST
HIGH = lax.Precision.HIGH


def shifted(x, axis, shift, devices):
    pairs = [(i, i + shift) for i in range(devices - shift)]
    return lax.ppermute(x, axis, pairs)


def ring(x, step):
    size = lax.axis_size("tensor")
    return lax.ppermute(x, "tensor", [(i, (i + step) % size) for i in range(size)])


def gathered(local):
    half = local.shape[0] // 2
    left_a = ring(local[:half], 1)
    right_a = ring(local[half:], -1)
    left_a, right_a, rest = lax.optimization_barrier((left_a, right_a, local))
    left_b = ring(rest[half:], 1)
    right_b = ring(rest[:half], -1)
    far = jnp.concatenate([ring(left_a, 1), ring(right_a, -1)])
    from_left = jnp.concatenate([left_a, left_b])
    from_right = jnp.concatenate([right_b, right_a])
    return jnp.concatenate([local, from_right, from_left], axis=1), far


def projected(near, far, weights):
    size = lax.axis_size("tensor")
    index = lax.axis_index("tensor")
    width = far.shape[1]
    parts = []
    for weight in weights:

        def rows(offset):
            return lax.dynamic_slice_in_dim(weight, ((index + offset) % size) * width, width, 0)

        near_rows = jnp.concatenate([rows(0), rows(1), rows(size - 1)])
        out = jnp.dot(near, near_rows, preferred_element_type=jnp.float32)
        parts.append(out + jnp.dot(far, rows(2), preferred_element_type=jnp.float32))
    return parts


def scattered_sum(gated, w_out):
    size = lax.axis_size("tensor")
    index = lax.axis_index("tensor")
    width = w_out.shape[1] // size
    rows = gated.shape[0]
    half = rows // 2

    def term(offset):
        cols = lax.dynamic_slice_in_dim(w_out, ((index + offset) % size) * width, width, 1)
        return jnp.dot(gated, cols, preferred_element_type=jnp.float32).astype(jnp.bfloat16)

    far = term(2)
    far_from_left = ring(far[:half], 1).astype(jnp.float32)
    far_from_right = ring(far[half:], -1).astype(jnp.float32)
    near_right, near_left = term(1), term(-1)
    to_right = jnp.concatenate(
        [(near_right[:half].astype(jnp.float32) + far_from_left).astype(jnp.bfloat16), near_right[half:]]
    )
    to_left = jnp.concatenate(
        [near_left[:half], (near_left[half:].astype(jnp.float32) + far_from_right).astype(jnp.bfloat16)]
    )
    from_left = ring(to_right, 1)
    from_right = ring(to_left, -1)
    total = term(0).astype(jnp.float32) + from_left.astype(jnp.float32)
    total = total + from_right.astype(jnp.float32)
    return total


def body(
    hidden_in,
    segment,
    w_query,
    w_key,
    w_value,
    w_outgate,
    w_gate_down,
    w_gate_up,
    gate_bias,
    norm_gain,
    w_out,
):
    tok_rows = hidden_in.shape[0]
    key_width = w_query.shape[1]
    value_width = w_value.shape[1]
    weights = (w_query, w_key, w_value, w_outgate, w_gate_down)
    query_sum, key_sum, value_sum, outgate, low = projected(*gathered(hidden_in), weights)
    query = query_sum.astype(jnp.bfloat16)
    key = key_sum.astype(jnp.bfloat16)
    value = value_sum.astype(jnp.bfloat16)
    pre_gate = jnp.dot(low, w_gate_up.astype(jnp.float32), precision=HIGHEST) + gate_bias
    logdecay = jax.nn.log_sigmoid(pre_gate) / 16.0

    blocks = tok_rows // GROUP
    starts = jnp.concatenate(
        [jnp.zeros((1,), jnp.int32), (segment[1:] != segment[:-1]).astype(jnp.int32)]
    )
    live_device = (jnp.cumsum(starts) == 0).astype(jnp.float32)
    seg_blocks = segment.reshape(blocks, GROUP)
    live_blocks = (jnp.cumsum(starts.reshape(blocks, GROUP), axis=1) == 0).astype(jnp.float32)
    cumul = jnp.cumsum(logdecay.reshape(blocks, GROUP, key_width), axis=1)
    block_totals = cumul[:, -1, :]
    before = jnp.cumsum(block_totals, axis=0) - block_totals
    device_cumul = (cumul + before[:, None, :]).reshape(tok_rows, key_width)

    q_float = query.astype(jnp.float32).reshape(blocks, GROUP, key_width)
    k_float = key.astype(jnp.float32).reshape(blocks, GROUP, key_width)
    v_blocks = value.reshape(blocks, GROUP, value_width)

    positions = jnp.arange(GROUP)
    causal = positions[None, :] <= positions[:, None]
    centre = cumul[:, GROUP // 2, :]
    q_scaled = q_float * jnp.exp(cumul - centre[:, None, :])
    k_scaled = k_float * jnp.exp(centre[:, None, :] - cumul)
    raw_scores = jnp.einsum(
        "ncd,nsd->ncs",
        q_scaled.astype(jnp.bfloat16),
        k_scaled.astype(jnp.bfloat16),
        preferred_element_type=jnp.float32,
    )
    allowed = causal[None] & (seg_blocks[:, :, None] == seg_blocks[:, None, :])
    scores = jnp.where(allowed, raw_scores, 0.0)
    intra = jnp.einsum(
        "ncs,nsv->ncv", scores.astype(jnp.bfloat16), v_blocks, preferred_element_type=jnp.float32
    )

    same_last = (seg_blocks == seg_blocks[:, -1:]).astype(jnp.float32)
    k_decayed = k_float * jnp.exp(block_totals[:, None, :] - cumul) * same_last[:, :, None]
    chunk_states = jnp.einsum(
        "ncd,ncv->ndv", k_decayed.astype(jnp.bfloat16), v_blocks, preferred_element_type=jnp.float32
    )
    chunk_decay = jnp.exp(block_totals) * live_blocks[:, -1:]

    q_decayed = q_float * jnp.exp(cumul)
    entering = jnp.zeros((key_width, value_width), jnp.float32)
    inters = []
    for n in range(blocks):
        inters.append(
            jnp.dot(
                q_decayed[n].astype(jnp.bfloat16),
                entering.astype(jnp.bfloat16),
                preferred_element_type=jnp.float32,
            )
        )
        entering = chunk_decay[n][:, None] * entering + chunk_states[n]
    final_state = entering
    inter = jnp.stack(inters) * live_blocks[:, :, None]
    local_out = (intra + inter).reshape(tok_rows, value_width)

    devices = lax.axis_size("req")
    window = min(devices - 1, -(-SEG_MOST // tok_rows))
    first_id = (segment[0] + 1).astype(jnp.float32)
    last_id = (segment[-1] + 1).astype(jnp.float32)
    decay_device = jnp.exp(device_cumul[-1]) * live_device[-1]
    tail = jnp.zeros((2, value_width), jnp.float32)
    tail = tail.at[0, :key_width].set(decay_device).at[1, 0].set(first_id).at[1, 1].set(last_id)
    message = jnp.concatenate([final_state, tail]).astype(jnp.bfloat16)
    def unpack(msg):
        return msg[:key_width], msg[key_width, :key_width], msg[key_width + 1, 0], msg[key_width + 1, 1]

    def joined(earlier, later):
        state_a, decay_a, first_a, last_a = earlier
        state_b, decay_b, first_b, last_b = later
        link = (first_b == last_a).astype(jnp.float32)
        return (state_b + (link * decay_b)[:, None] * state_a, decay_a * decay_b * link, first_a, last_b)

    assert window == 4
    pair = joined(
        unpack(shifted(message, "req", 2, devices).astype(jnp.float32)),
        unpack(shifted(message, "req", 1, devices).astype(jnp.float32)),
    )
    pair_state, pair_decay, pair_first, pair_last = pair
    pair_tail = jnp.zeros((2, value_width), jnp.float32)
    pair_tail = pair_tail.at[0, :key_width].set(pair_decay).at[1, 0].set(pair_first)
    pair_tail = pair_tail.at[1, 1].set(pair_last)
    pair_message = jnp.concatenate([pair_state, pair_tail]).astype(jnp.bfloat16)
    earlier_pair = unpack(shifted(pair_message, "req", 2, devices).astype(jnp.float32))
    state_in, _, _, last_far = joined(earlier_pair, pair)
    linked = (first_id == last_far).astype(jnp.float32)
    carried = jnp.dot(
        (query.astype(jnp.float32) * jnp.exp(device_cumul)).astype(jnp.bfloat16),
        state_in.astype(jnp.bfloat16),
        preferred_element_type=jnp.float32,
    )
    attn = (local_out + carried * (live_device * linked)[:, None]) * key_width ** (-0.5)
    normed = attn * lax.rsqrt(jnp.mean(attn * attn, axis=-1, keepdims=True) + 1e-05) * norm_gain
    gated = (normed * jax.nn.silu(outgate)).astype(jnp.bfloat16)
    return scattered_sum(gated, w_out).astype(jnp.bfloat16)


def solution(mesh):
    in_specs = (
        P("req", "tensor"),
        P("req"),
        P(None, "tensor"),
        P(None, "tensor"),
        P(None, "tensor"),
        P(None, "tensor"),
        P(),
        P(None, "tensor"),
        P("tensor"),
        P(),
        P("tensor", None),
    )
    out_specs = P("req", "tensor")
    return jax.shard_map(body, mesh=mesh, in_specs=in_specs, out_specs=out_specs, check_vma=False)
```

```python
import jax
import jax.numpy as jnp
from jax import lax
from jax.sharding import PartitionSpec as P

GROUP = 64
SEG_MOST = 4096
HIGHEST = lax.Precision.HIGHEST
HIGH = lax.Precision.HIGH


def shifted(x, axis, shift, devices):
    pairs = [(i, i + shift) for i in range(devices - shift)]
    return lax.ppermute(x, axis, pairs)


def ring(x, step):
    size = lax.axis_size("tensor")
    return lax.ppermute(x, "tensor", [(i, (i + step) % size) for i in range(size)])


def gathered(local):
    half = local.shape[0] // 2
    left_a = ring(local[:half], 1)
    right_a = ring(local[half:], -1)
    left_a, right_a, rest = lax.optimization_barrier((left_a, right_a, local))
    left_b = ring(rest[half:], 1)
    right_b = ring(rest[:half], -1)
    far = jnp.concatenate([ring(left_a, 1), ring(right_a, -1)])
    from_left = jnp.concatenate([left_a, left_b])
    from_right = jnp.concatenate([right_b, right_a])
    return jnp.concatenate([local, from_right, from_left], axis=1), far


def projected(near, far, weights):
    size = lax.axis_size("tensor")
    index = lax.axis_index("tensor")
    width = far.shape[1]
    parts = []
    for weight in weights:

        def rows(offset):
            return lax.dynamic_slice_in_dim(weight, ((index + offset) % size) * width, width, 0)

        near_rows = jnp.concatenate([rows(0), rows(1), rows(size - 1)])
        out = jnp.dot(near, near_rows, preferred_element_type=jnp.float32)
        parts.append(out + jnp.dot(far, rows(2), preferred_element_type=jnp.float32))
    return parts


def scattered_sum(gated, w_out):
    size = lax.axis_size("tensor")
    index = lax.axis_index("tensor")
    width = w_out.shape[1] // size
    rows = gated.shape[0]
    half = rows // 2

    def term(offset):
        cols = lax.dynamic_slice_in_dim(w_out, ((index + offset) % size) * width, width, 1)
        return jnp.dot(gated, cols, preferred_element_type=jnp.float32).astype(jnp.bfloat16)

    far_cols = lax.dynamic_slice_in_dim(w_out, ((index + 2) % size) * width, width, 1)
    far_top = jnp.dot(gated[:half], far_cols, preferred_element_type=jnp.float32)
    far_from_left = ring(far_top.astype(jnp.bfloat16), 1).astype(jnp.float32)
    far_bottom = jnp.dot(gated[half:], far_cols, preferred_element_type=jnp.float32)
    far_from_right = ring(far_bottom.astype(jnp.bfloat16), -1).astype(jnp.float32)
    near_right, near_left = term(1), term(-1)
    to_right = jnp.concatenate(
        [(near_right[:half].astype(jnp.float32) + far_from_left).astype(jnp.bfloat16), near_right[half:]]
    )
    to_left = jnp.concatenate(
        [near_left[:half], (near_left[half:].astype(jnp.float32) + far_from_right).astype(jnp.bfloat16)]
    )
    from_left = ring(to_right, 1)
    from_right = ring(to_left, -1)
    total = term(0).astype(jnp.float32) + from_left.astype(jnp.float32)
    total = total + from_right.astype(jnp.float32)
    return total


def body(
    hidden_in,
    segment,
    w_query,
    w_key,
    w_value,
    w_outgate,
    w_gate_down,
    w_gate_up,
    gate_bias,
    norm_gain,
    w_out,
):
    tok_rows = hidden_in.shape[0]
    key_width = w_query.shape[1]
    value_width = w_value.shape[1]
    weights = (w_query, w_key, w_value, w_outgate, w_gate_down)
    query_sum, key_sum, value_sum, outgate, low = projected(*gathered(hidden_in), weights)
    query = query_sum.astype(jnp.bfloat16)
    key = key_sum.astype(jnp.bfloat16)
    value = value_sum.astype(jnp.bfloat16)
    pre_gate = jnp.dot(low, w_gate_up.astype(jnp.float32), precision=HIGHEST) + gate_bias
    logdecay = jax.nn.log_sigmoid(pre_gate) / 16.0

    blocks = tok_rows // GROUP
    starts = jnp.concatenate(
        [jnp.zeros((1,), jnp.int32), (segment[1:] != segment[:-1]).astype(jnp.int32)]
    )
    live_device = (jnp.cumsum(starts) == 0).astype(jnp.float32)
    seg_blocks = segment.reshape(blocks, GROUP)
    live_blocks = (jnp.cumsum(starts.reshape(blocks, GROUP), axis=1) == 0).astype(jnp.float32)
    cumul = jnp.cumsum(logdecay.reshape(blocks, GROUP, key_width), axis=1)
    block_totals = cumul[:, -1, :]
    before = jnp.cumsum(block_totals, axis=0) - block_totals
    device_cumul = (cumul + before[:, None, :]).reshape(tok_rows, key_width)

    q_float = query.astype(jnp.float32).reshape(blocks, GROUP, key_width)
    k_float = key.astype(jnp.float32).reshape(blocks, GROUP, key_width)
    v_float = value.astype(jnp.float32).reshape(blocks, GROUP, value_width)

    positions = jnp.arange(GROUP)
    causal = positions[None, :] <= positions[:, None]
    centre = cumul[:, GROUP // 2, :]
    q_scaled = q_float * jnp.exp(cumul - centre[:, None, :])
    k_scaled = k_float * jnp.exp(centre[:, None, :] - cumul)
    raw_scores = jnp.einsum(
        "ncd,nsd->ncs",
        q_scaled.astype(jnp.bfloat16),
        k_scaled.astype(jnp.bfloat16),
        preferred_element_type=jnp.float32,
    )
    allowed = causal[None] & (seg_blocks[:, :, None] == seg_blocks[:, None, :])
    scores = jnp.where(allowed, raw_scores, 0.0)
    intra = jnp.einsum("ncs,nsv->ncv", scores, v_float, precision=HIGH)

    same_last = (seg_blocks == seg_blocks[:, -1:]).astype(jnp.float32)
    k_decayed = k_float * jnp.exp(block_totals[:, None, :] - cumul) * same_last[:, :, None]
    chunk_states = jnp.einsum("ncd,ncv->ndv", k_decayed, v_float, precision=HIGH)
    chunk_decay = jnp.exp(block_totals) * live_blocks[:, -1:]

    q_decayed = q_float * jnp.exp(cumul)
    entering = jnp.zeros((key_width, value_width), jnp.float32)
    inters = []
    for n in range(blocks):
        inters.append(
            jnp.dot(
                q_decayed[n].astype(jnp.bfloat16),
                entering.astype(jnp.bfloat16),
                preferred_element_type=jnp.float32,
            )
        )
        entering = chunk_decay[n][:, None] * entering + chunk_states[n]
    final_state = entering
    inter = jnp.stack(inters) * live_blocks[:, :, None]
    local_out = (intra + inter).reshape(tok_rows, value_width)

    devices = lax.axis_size("req")
    window = min(devices - 1, -(-SEG_MOST // tok_rows))
    first_id = (segment[0] + 1).astype(jnp.float32)
    last_id = (segment[-1] + 1).astype(jnp.float32)
    decay_device = jnp.exp(device_cumul[-1]) * live_device[-1]
    tail = jnp.zeros((2, value_width), jnp.float32)
    tail = tail.at[0, :key_width].set(decay_device).at[1, 0].set(first_id).at[1, 1].set(last_id)
    message = jnp.concatenate([final_state, tail]).astype(jnp.bfloat16)
    def unpack(msg):
        return msg[:key_width], msg[key_width, :key_width], msg[key_width + 1, 0], msg[key_width + 1, 1]

    def joined(earlier, later):
        state_a, decay_a, first_a, last_a = earlier
        state_b, decay_b, first_b, last_b = later
        link = (first_b == last_a).astype(jnp.float32)
        return (state_b + (link * decay_b)[:, None] * state_a, decay_a * decay_b * link, first_a, last_b)

    assert window == 4
    pair = joined(
        unpack(shifted(message, "req", 2, devices).astype(jnp.float32)),
        unpack(shifted(message, "req", 1, devices).astype(jnp.float32)),
    )
    pair_state, pair_decay, pair_first, pair_last = pair
    pair_tail = jnp.zeros((2, value_width), jnp.float32)
    pair_tail = pair_tail.at[0, :key_width].set(pair_decay).at[1, 0].set(pair_first)
    pair_tail = pair_tail.at[1, 1].set(pair_last)
    pair_message = jnp.concatenate([pair_state, pair_tail]).astype(jnp.bfloat16)
    earlier_pair = unpack(shifted(pair_message, "req", 2, devices).astype(jnp.float32))
    state_in, _, _, last_far = joined(earlier_pair, pair)
    linked = (first_id == last_far).astype(jnp.float32)
    carried = jnp.dot(
        (query.astype(jnp.float32) * jnp.exp(device_cumul)).astype(jnp.bfloat16),
        state_in.astype(jnp.bfloat16),
        preferred_element_type=jnp.float32,
    )
    attn = (local_out + carried * (live_device * linked)[:, None]) * key_width ** (-0.5)
    normed = attn * lax.rsqrt(jnp.mean(attn * attn, axis=-1, keepdims=True) + 1e-05) * norm_gain
    gated = (normed * jax.nn.silu(outgate)).astype(jnp.bfloat16)
    return scattered_sum(gated, w_out).astype(jnp.bfloat16)


def solution(mesh):
    in_specs = (
        P("req", "tensor"),
        P("req"),
        P(None, "tensor"),
        P(None, "tensor"),
        P(None, "tensor"),
        P(None, "tensor"),
        P(),
        P(None, "tensor"),
        P("tensor"),
        P(),
        P("tensor", None),
    )
    out_specs = P("req", "tensor")
    return jax.shard_map(body, mesh=mesh, in_specs=in_specs, out_specs=out_specs, check_vma=False)
```

```python
import jax
import jax.numpy as jnp
from jax import lax
from jax.sharding import PartitionSpec as P

GROUP = 64
SEG_MOST = 4096
HIGHEST = lax.Precision.HIGHEST
HIGH = lax.Precision.HIGH


def shifted(x, axis, shift, devices):
    pairs = [(i, i + shift) for i in range(devices - shift)]
    return lax.ppermute(x, axis, pairs)


def ring(x, step):
    size = lax.axis_size("tensor")
    return lax.ppermute(x, "tensor", [(i, (i + step) % size) for i in range(size)])


def gathered(local):
    half = local.shape[0] // 2
    from_left = ring(local, 1)
    from_right = ring(local, -1)
    far = jnp.concatenate([ring(from_left[:half], 1), ring(from_right[half:], -1)])
    return jnp.concatenate([local, from_right, from_left], axis=1), far


def projected(near, far, weights):
    size = lax.axis_size("tensor")
    index = lax.axis_index("tensor")
    width = far.shape[1]
    parts = []
    for weight in weights:

        def rows(offset):
            return lax.dynamic_slice_in_dim(weight, ((index + offset) % size) * width, width, 0)

        near_rows = jnp.concatenate([rows(0), rows(1), rows(size - 1)])
        out = jnp.dot(near, near_rows, preferred_element_type=jnp.float32)
        parts.append(out + jnp.dot(far, rows(2), preferred_element_type=jnp.float32))
    return parts


def scattered_sum(gated, w_out):
    size = lax.axis_size("tensor")
    index = lax.axis_index("tensor")
    width = w_out.shape[1] // size
    rows = gated.shape[0]
    half = rows // 2

    def term(offset):
        cols = lax.dynamic_slice_in_dim(w_out, ((index + offset) % size) * width, width, 1)
        return jnp.dot(gated, cols, preferred_element_type=jnp.float32).astype(jnp.bfloat16)

    far = term(2)
    far_from_left = ring(far[:half], 1).astype(jnp.float32)
    far_from_right = ring(far[half:], -1).astype(jnp.float32)
    near_right, near_left = term(1), term(-1)
    to_right = jnp.concatenate(
        [(near_right[:half].astype(jnp.float32) + far_from_left).astype(jnp.bfloat16), near_right[half:]]
    )
    to_left = jnp.concatenate(
        [near_left[:half], (near_left[half:].astype(jnp.float32) + far_from_right).astype(jnp.bfloat16)]
    )
    from_left = ring(to_right, 1)
    from_right = ring(to_left, -1)
    total = term(0).astype(jnp.float32) + from_left.astype(jnp.float32)
    total = total + from_right.astype(jnp.float32)
    return total


def body(
    hidden_in,
    segment,
    w_query,
    w_key,
    w_value,
    w_outgate,
    w_gate_down,
    w_gate_up,
    gate_bias,
    norm_gain,
    w_out,
):
    tok_rows = hidden_in.shape[0]
    key_width = w_query.shape[1]
    value_width = w_value.shape[1]
    weights = (w_query, w_key, w_value, w_outgate, w_gate_down)
    query_sum, key_sum, value_sum, outgate, low = projected(*gathered(hidden_in), weights)
    query = query_sum.astype(jnp.bfloat16)
    key = key_sum.astype(jnp.bfloat16)
    value = value_sum.astype(jnp.bfloat16)
    pre_gate = jnp.dot(low, w_gate_up.astype(jnp.float32), precision=HIGHEST) + gate_bias
    logdecay = jax.nn.log_sigmoid(pre_gate) / 16.0

    blocks = tok_rows // GROUP
    starts = jnp.concatenate(
        [jnp.zeros((1,), jnp.int32), (segment[1:] != segment[:-1]).astype(jnp.int32)]
    )
    live_device = (jnp.cumsum(starts) == 0).astype(jnp.float32)
    seg_blocks = segment.reshape(blocks, GROUP)
    live_blocks = (jnp.cumsum(starts.reshape(blocks, GROUP), axis=1) == 0).astype(jnp.float32)
    cumul = jnp.cumsum(logdecay.reshape(blocks, GROUP, key_width), axis=1)
    block_totals = cumul[:, -1, :]
    before = jnp.cumsum(block_totals, axis=0) - block_totals
    device_cumul = (cumul + before[:, None, :]).reshape(tok_rows, key_width)

    q_float = query.astype(jnp.float32).reshape(blocks, GROUP, key_width)
    k_float = key.astype(jnp.float32).reshape(blocks, GROUP, key_width)
    v_float = value.astype(jnp.float32).reshape(blocks, GROUP, value_width)

    positions = jnp.arange(GROUP)
    causal = positions[None, :] <= positions[:, None]
    centre = cumul[:, GROUP // 2, :]
    q_scaled = q_float * jnp.exp(cumul - centre[:, None, :])
    k_scaled = k_float * jnp.exp(centre[:, None, :] - cumul)
    raw_scores = jnp.einsum(
        "ncd,nsd->ncs",
        q_scaled.astype(jnp.bfloat16),
        k_scaled.astype(jnp.bfloat16),
        preferred_element_type=jnp.float32,
    )
    allowed = causal[None] & (seg_blocks[:, :, None] == seg_blocks[:, None, :])
    scores = jnp.where(allowed, raw_scores, 0.0)
    intra = jnp.einsum("ncs,nsv->ncv", scores, v_float, precision=HIGH)

    same_last = (seg_blocks == seg_blocks[:, -1:]).astype(jnp.float32)
    k_decayed = k_float * jnp.exp(block_totals[:, None, :] - cumul) * same_last[:, :, None]
    chunk_states = jnp.einsum("ncd,ncv->ndv", k_decayed, v_float, precision=HIGH)
    chunk_decay = jnp.exp(block_totals) * live_blocks[:, -1:]

    q_decayed = q_float * jnp.exp(cumul)
    entering = jnp.zeros((key_width, value_width), jnp.float32)
    inters = []
    for n in range(blocks):
        inters.append(
            jnp.dot(
                q_decayed[n].astype(jnp.bfloat16),
                entering.astype(jnp.bfloat16),
                preferred_element_type=jnp.float32,
            )
        )
        entering = chunk_decay[n][:, None] * entering + chunk_states[n]
    final_state = entering
    inter = jnp.stack(inters) * live_blocks[:, :, None]
    local_out = (intra + inter).reshape(tok_rows, value_width)

    devices = lax.axis_size("req")
    window = min(devices - 1, -(-SEG_MOST // tok_rows))
    first_id = (segment[0] + 1).astype(jnp.float32)
    last_id = (segment[-1] + 1).astype(jnp.float32)
    decay_device = jnp.exp(device_cumul[-1]) * live_device[-1]
    tail = jnp.zeros((2, value_width), jnp.float32)
    tail = tail.at[0, :key_width].set(decay_device).at[1, 0].set(first_id).at[1, 1].set(last_id)
    message = jnp.concatenate([final_state, tail]).astype(jnp.bfloat16)
    def unpack(msg):
        return msg[:key_width], msg[key_width, :key_width], msg[key_width + 1, 0], msg[key_width + 1, 1]

    def joined(earlier, later):
        state_a, decay_a, first_a, last_a = earlier
        state_b, decay_b, first_b, last_b = later
        link = (first_b == last_a).astype(jnp.float32)
        return (state_b + (link * decay_b)[:, None] * state_a, decay_a * decay_b * link, first_a, last_b)

    assert window == 4
    pair = joined(
        unpack(shifted(message, "req", 2, devices).astype(jnp.float32)),
        unpack(shifted(message, "req", 1, devices).astype(jnp.float32)),
    )
    pair_state, pair_decay, pair_first, pair_last = pair
    pair_tail = jnp.zeros((2, value_width), jnp.float32)
    pair_tail = pair_tail.at[0, :key_width].set(pair_decay).at[1, 0].set(pair_first)
    pair_tail = pair_tail.at[1, 1].set(pair_last)
    pair_message = jnp.concatenate([pair_state, pair_tail]).astype(jnp.bfloat16)
    earlier_pair = unpack(shifted(pair_message, "req", 2, devices).astype(jnp.float32))
    state_in, _, _, last_far = joined(earlier_pair, pair)
    linked = (first_id == last_far).astype(jnp.float32)
    carried = jnp.dot(
        (query.astype(jnp.float32) * jnp.exp(device_cumul)).astype(jnp.bfloat16),
        state_in.astype(jnp.bfloat16),
        preferred_element_type=jnp.float32,
    )
    attn = (local_out + carried * (live_device * linked)[:, None]) * key_width ** (-0.5)
    normed = attn * lax.rsqrt(jnp.mean(attn * attn, axis=-1, keepdims=True) + 1e-05) * norm_gain
    gated = (normed * jax.nn.silu(outgate)).astype(jnp.bfloat16)
    return scattered_sum(gated, w_out).astype(jnp.bfloat16)


def solution(mesh):
    in_specs = (
        P("req", "tensor"),
        P("req"),
        P(None, "tensor"),
        P(None, "tensor"),
        P(None, "tensor"),
        P(None, "tensor"),
        P(),
        P(None, "tensor"),
        P("tensor"),
        P(),
        P("tensor", None),
    )
    out_specs = P("req", "tensor")
    return jax.shard_map(body, mesh=mesh, in_specs=in_specs, out_specs=out_specs, check_vma=False)
```

```python
import jax
import jax.numpy as jnp
from jax import lax
from jax.sharding import PartitionSpec as P

GROUP = 64
SEG_MOST = 4096
HIGHEST = lax.Precision.HIGHEST
HIGH = lax.Precision.HIGH


def shifted(x, axis, shift, devices):
    pairs = [(i, i + shift) for i in range(devices - shift)]
    return lax.ppermute(x, axis, pairs)


def ring(x, step):
    size = lax.axis_size("tensor")
    return lax.ppermute(x, "tensor", [(i, (i + step) % size) for i in range(size)])


def gathered(local):
    half = local.shape[0] // 2
    left_a = ring(local[:half], 1)
    right_a = ring(local[half:], -1)
    left_a, right_a, rest = lax.optimization_barrier((left_a, right_a, local))
    left_b = ring(rest[half:], 1)
    right_b = ring(rest[:half], -1)
    far = jnp.concatenate([ring(left_a, 1), ring(right_a, -1)])
    from_left = jnp.concatenate([left_a, left_b])
    from_right = jnp.concatenate([right_b, right_a])
    return jnp.concatenate([local, from_right, from_left], axis=1), far


def projected(near, far, weights):
    size = lax.axis_size("tensor")
    index = lax.axis_index("tensor")
    width = far.shape[1]
    parts = []
    for weight in weights:

        def rows(offset):
            return lax.dynamic_slice_in_dim(weight, ((index + offset) % size) * width, width, 0)

        near_rows = jnp.concatenate([rows(0), rows(1), rows(size - 1)])
        out = jnp.dot(near, near_rows, preferred_element_type=jnp.float32)
        parts.append(out + jnp.dot(far, rows(2), preferred_element_type=jnp.float32))
    return parts


def scattered_sum(gated, w_out):
    size = lax.axis_size("tensor")
    index = lax.axis_index("tensor")
    width = w_out.shape[1] // size
    rows = gated.shape[0]
    half = rows // 2

    def term(offset):
        cols = lax.dynamic_slice_in_dim(w_out, ((index + offset) % size) * width, width, 1)
        return jnp.dot(gated, cols, preferred_element_type=jnp.float32).astype(jnp.bfloat16)

    far = term(2)
    far_from_left = ring(far[:half], 1).astype(jnp.float32)
    far_from_right = ring(far[half:], -1).astype(jnp.float32)
    near_right, near_left = term(1), term(-1)
    to_right = jnp.concatenate(
        [(near_right[:half].astype(jnp.float32) + far_from_left).astype(jnp.bfloat16), near_right[half:]]
    )
    to_left = jnp.concatenate(
        [near_left[:half], (near_left[half:].astype(jnp.float32) + far_from_right).astype(jnp.bfloat16)]
    )
    from_left = ring(to_right, 1)
    from_right = ring(to_left, -1)
    total = term(0).astype(jnp.float32) + from_left.astype(jnp.float32)
    total = total + from_right.astype(jnp.float32)
    return total


def body(
    hidden_in,
    segment,
    w_query,
    w_key,
    w_value,
    w_outgate,
    w_gate_down,
    w_gate_up,
    gate_bias,
    norm_gain,
    w_out,
):
    tok_rows = hidden_in.shape[0]
    key_width = w_query.shape[1]
    value_width = w_value.shape[1]
    weights = (w_query, w_key, w_value, w_outgate, w_gate_down)
    query_sum, key_sum, value_sum, outgate, low = projected(*gathered(hidden_in), weights)
    query = query_sum.astype(jnp.bfloat16)
    key = key_sum.astype(jnp.bfloat16)
    value = value_sum.astype(jnp.bfloat16)
    pre_gate = jnp.dot(low, w_gate_up.astype(jnp.float32), precision=HIGHEST) + gate_bias
    logdecay = jax.nn.log_sigmoid(pre_gate) / 16.0

    blocks = tok_rows // GROUP
    starts = jnp.concatenate(
        [jnp.zeros((1,), jnp.int32), (segment[1:] != segment[:-1]).astype(jnp.int32)]
    )
    live_device = (jnp.cumsum(starts) == 0).astype(jnp.float32)
    seg_blocks = segment.reshape(blocks, GROUP)
    live_blocks = (jnp.cumsum(starts.reshape(blocks, GROUP), axis=1) == 0).astype(jnp.float32)
    cumul = jnp.cumsum(logdecay.reshape(blocks, GROUP, key_width), axis=1)
    block_totals = cumul[:, -1, :]
    before = jnp.cumsum(block_totals, axis=0) - block_totals
    device_cumul = (cumul + before[:, None, :]).reshape(tok_rows, key_width)

    q_float = query.astype(jnp.float32).reshape(blocks, GROUP, key_width)
    k_float = key.astype(jnp.float32).reshape(blocks, GROUP, key_width)
    v_float = value.astype(jnp.float32).reshape(blocks, GROUP, value_width)

    positions = jnp.arange(GROUP)
    causal = positions[None, :] <= positions[:, None]
    centre = cumul[:, GROUP // 2, :]
    q_scaled = q_float * jnp.exp(cumul - centre[:, None, :])
    k_scaled = k_float * jnp.exp(centre[:, None, :] - cumul)
    raw_scores = jnp.einsum(
        "ncd,nsd->ncs",
        q_scaled.astype(jnp.bfloat16),
        k_scaled.astype(jnp.bfloat16),
        preferred_element_type=jnp.float32,
    )
    allowed = causal[None] & (seg_blocks[:, :, None] == seg_blocks[:, None, :])
    scores = jnp.where(allowed, raw_scores, 0.0)
    intra = jnp.einsum("ncs,nsv->ncv", scores, v_float, precision=HIGH)

    same_last = (seg_blocks == seg_blocks[:, -1:]).astype(jnp.float32)
    k_decayed = k_float * jnp.exp(block_totals[:, None, :] - cumul) * same_last[:, :, None]
    chunk_states = jnp.einsum("ncd,ncv->ndv", k_decayed, v_float, precision=HIGH)
    chunk_decay = jnp.exp(block_totals) * live_blocks[:, -1:]

    q_decayed = q_float * jnp.exp(cumul)
    entering = jnp.zeros((key_width, value_width), jnp.float32)
    inters = []
    for n in range(blocks):
        inters.append(
            jnp.dot(
                q_decayed[n].astype(jnp.bfloat16),
                entering.astype(jnp.bfloat16),
                preferred_element_type=jnp.float32,
            )
        )
        entering = chunk_decay[n][:, None] * entering + chunk_states[n]
    final_state = entering
    local_out = jnp.concatenate(
        [intra[n] + inters[n] * live_blocks[n][:, None] for n in range(blocks)], axis=0
    )

    devices = lax.axis_size("req")
    window = min(devices - 1, -(-SEG_MOST // tok_rows))
    first_id = (segment[0] + 1).astype(jnp.float32)
    last_id = (segment[-1] + 1).astype(jnp.float32)
    decay_device = jnp.exp(device_cumul[-1]) * live_device[-1]
    tail = jnp.zeros((2, value_width), jnp.float32)
    tail = tail.at[0, :key_width].set(decay_device).at[1, 0].set(first_id).at[1, 1].set(last_id)
    message = jnp.concatenate([final_state, tail]).astype(jnp.bfloat16)
    def unpack(msg):
        return msg[:key_width], msg[key_width, :key_width], msg[key_width + 1, 0], msg[key_width + 1, 1]

    def joined(earlier, later):
        state_a, decay_a, first_a, last_a = earlier
        state_b, decay_b, first_b, last_b = later
        link = (first_b == last_a).astype(jnp.float32)
        return (state_b + (link * decay_b)[:, None] * state_a, decay_a * decay_b * link, first_a, last_b)

    assert window == 4
    pair = joined(
        unpack(shifted(message, "req", 2, devices).astype(jnp.float32)),
        unpack(shifted(message, "req", 1, devices).astype(jnp.float32)),
    )
    pair_state, pair_decay, pair_first, pair_last = pair
    pair_tail = jnp.zeros((2, value_width), jnp.float32)
    pair_tail = pair_tail.at[0, :key_width].set(pair_decay).at[1, 0].set(pair_first)
    pair_tail = pair_tail.at[1, 1].set(pair_last)
    pair_message = jnp.concatenate([pair_state, pair_tail]).astype(jnp.bfloat16)
    earlier_pair = unpack(shifted(pair_message, "req", 2, devices).astype(jnp.float32))
    state_in, _, _, last_far = joined(earlier_pair, pair)
    linked = (first_id == last_far).astype(jnp.float32)
    carried = jnp.dot(
        (query.astype(jnp.float32) * jnp.exp(device_cumul)).astype(jnp.bfloat16),
        state_in.astype(jnp.bfloat16),
        preferred_element_type=jnp.float32,
    )
    attn = (local_out + carried * (live_device * linked)[:, None]) * key_width ** (-0.5)
    normed = attn * lax.rsqrt(jnp.mean(attn * attn, axis=-1, keepdims=True) + 1e-05) * norm_gain
    gated = (normed * jax.nn.silu(outgate)).astype(jnp.bfloat16)
    return scattered_sum(gated, w_out).astype(jnp.bfloat16)


def solution(mesh):
    in_specs = (
        P("req", "tensor"),
        P("req"),
        P(None, "tensor"),
        P(None, "tensor"),
        P(None, "tensor"),
        P(None, "tensor"),
        P(),
        P(None, "tensor"),
        P("tensor"),
        P(),
        P("tensor", None),
    )
    out_specs = P("req", "tensor")
    return jax.shard_map(body, mesh=mesh, in_specs=in_specs, out_specs=out_specs, check_vma=False)
```
